128 devices in a mesh: site: 4 (over y_lo, core), section: 4 (over x), tensor: 8 (over y_hi, z).
Axes of the slice: x: 4, y: 4 (y_hi: 2, y_lo: 2; y = y_hi * 2 + y_lo), z: 4, core: 2. Of those that a mesh axis runs over, the one named last changes fastest.
Arguments:
- inputs: bfloat16 [4, 4, 256, 896], P('site'), may hold values from -6 to 6
- out_grad: bfloat16 [4, 4, 256, 896], P('site'), may hold values from -0.1875 to 0.1875
- local_gate: bfloat16 [4, 4, 896, 4864], P('site', 'section', None, 'tensor'), may hold values from -0.1875 to 0.1875
- local_up: bfloat16 [4, 4, 896, 4864], P('site', 'section', None, 'tensor'), may hold values from -0.1875 to 0.1875
- local_down: bfloat16 [4, 4, 4864, 896], P('site', 'section', 'tensor'), may hold values from -0.078125 to 0.078125
- local_gain: float32 [4, 4, 896], P('site', 'section'), may hold values from 0.5 to 1.5
- anchor_gate: bfloat16 [4, 896, 4864], P('section', None, 'tensor'), may hold values from -0.1875 to 0.1875
- anchor_up: bfloat16 [4, 896, 4864], P('section', None, 'tensor'), may hold values from -0.1875 to 0.1875
- anchor_down: bfloat16 [4, 4864, 896], P('section', 'tensor'), may hold values from -0.078125 to 0.078125
- anchor_gain: float32 [4, 896], P('section'), may hold values from 0.5 to 1.5
Outputs:
- round_gate: float32 [4, 896, 4864], P('section', None, 'tensor')
- round_up: float32 [4, 896, 4864], P('section', None, 'tensor')
- round_down: float32 [4, 4864, 896], P('section', 'tensor')
- round_gain: float32 [4, 896], P('section')
The draws below stay inside these ranges and needn't reach their ends.
All inputs are finite; a program needn't handle non-finite values.
Results may differ from the reference program's by a relative error of at most 0.03.
Values may be sent and summed in bfloat16 or wider, within the bound.
No kernel may reach another device: no remote copies, remote signals or barrier semaphores. Data moves between devices by JAX's collectives and lax.ppermute only.
A program may use at most 128 MiB of HBM per device.

```python
import jax
import jax.numpy as jnp
from jax import lax

D = 896
FF = 4864
ROWS = 256
MICRO = 4
SITES = 4
SECTIONS = 4
N_SITE = 4
N_SECTION = 4
N_TENSOR = 8


def steps_of(key, dims, split, smallest, largest):
    level = 1.0
    for position, shards_of in split:
        steps = jax.random.uniform(jax.random.fold_in(jax.random.fold_in(key, 6), position), (shards_of,), jnp.float32, smallest / len(split), largest / len(split))
        level = level * jnp.repeat(jnp.exp(steps), dims[position] // shards_of).reshape((-1,) + (1,) * (len(dims) - 1 - position))
    return level


def bell_draw(rng, dims, scale, most, cuts=(), held_as=jnp.bfloat16):
    drawn = scale * jax.random.normal(rng, dims, jnp.float32)
    if cuts:
        drawn = drawn * steps_of(rng, dims, cuts, -0.22, 0.18)
    return jnp.clip(drawn, -most, most).astype(held_as)


def setup_inputs(seed: int = 0) -> dict:
    seeds = jax.random.split(jax.random.key(seed), 11)
    return {
        "inputs": bell_draw(seeds[0], (SITES, MICRO, ROWS, D), 1.0, 6.0, ((0, 4),)),
        "out_grad": bell_draw(seeds[1], (SITES, MICRO, ROWS, D), 0.03125, 0.1875, ((0, 4),)),
        "local_gate": bell_draw(seeds[2], (SITES, SECTIONS, D, FF), D ** -0.5, 0.1875, ((0, 4), (1, 4), (3, 8))),
        "local_up": bell_draw(seeds[3], (SITES, SECTIONS, D, FF), D ** -0.5, 0.1875, ((0, 4), (1, 4), (3, 8))),
        "local_down": bell_draw(seeds[4], (SITES, SECTIONS, FF, D), FF ** -0.5, 0.078125, ((0, 4), (1, 4), (2, 8))),
        "local_gain": jnp.clip(1.0 + 0.1 * jax.random.normal(seeds[5], (SITES, SECTIONS, D), jnp.float32), 0.5, 1.5),
        "anchor_gate": bell_draw(seeds[6], (SECTIONS, D, FF), D ** -0.5, 0.1875, ((0, 4), (2, 8))),
        "anchor_up": bell_draw(seeds[7], (SECTIONS, D, FF), D ** -0.5, 0.1875, ((0, 4), (2, 8))),
        "anchor_down": bell_draw(seeds[8], (SECTIONS, FF, D), FF ** -0.5, 0.078125, ((0, 4), (1, 8))),
        "anchor_gain": jnp.clip(1.0 + 0.1 * jax.random.normal(seeds[9], (SECTIONS, D), jnp.float32), 0.5, 1.5),
    }


epsilon = 1e-06
prox_weight = 1.0

def norm_rows(wide_rows, gain_row):
    row_scale = lax.rsqrt(lax.optimization_barrier(jnp.mean(wide_rows * wide_rows, axis=-1, keepdims=True)) + epsilon)
    unit_rows = wide_rows * row_scale
    return (unit_rows, row_scale, (unit_rows * gain_row).astype(jnp.bfloat16))

def rounded_blocks(block_terms):
    held_terms = block_terms.astype(jnp.bfloat16)
    held_terms = lax.optimization_barrier(held_terms)
    return lax.optimization_barrier(jnp.sum(held_terms.astype(jnp.float32), axis=0))

def down_blocks(hidden, w_down):
    row_total = hidden.shape[0]
    blocked = hidden.astype(jnp.float32).reshape(row_total, N_TENSOR, -1)
    weights = w_down.astype(jnp.float32).reshape(N_TENSOR, -1, w_down.shape[1])
    return rounded_blocks(jnp.einsum('rtf,tfd->trd', blocked, weights))

def input_blocks(d_gate_pre, d_up_pre, w_gate, w_up):
    row_total = d_gate_pre.shape[0]
    gate_blocks = d_gate_pre.astype(jnp.float32).reshape(row_total, N_TENSOR, -1)
    up_blocks = d_up_pre.astype(jnp.float32).reshape(row_total, N_TENSOR, -1)
    gate_weights = w_gate.astype(jnp.float32).reshape(w_gate.shape[0], N_TENSOR, -1)
    up_weights = w_up.astype(jnp.float32).reshape(w_up.shape[0], N_TENSOR, -1)
    block_terms = jnp.einsum('rtf,dtf->trd', gate_blocks, gate_weights) + jnp.einsum('rtf,dtf->trd', up_blocks, up_weights)
    return rounded_blocks(block_terms)

def site_gradients(site_feed, loss_grad, w_gates, w_ups, w_downs, gains):
    section_acts = site_feed.reshape(-1, D)
    stored = []
    for section_index in range(N_SECTION):
        stored.append(section_acts)
        wide_in = section_acts.astype(jnp.float32)
        unit_rows, row_scale, normed = norm_rows(wide_in, gains[section_index])
        gate_pre = jnp.dot(normed, w_gates[section_index], preferred_element_type=jnp.float32)
        up_pre = jnp.dot(normed, w_ups[section_index], preferred_element_type=jnp.float32)
        hidden = (gate_pre * jax.nn.sigmoid(gate_pre) * up_pre).astype(jnp.bfloat16)
        section_acts = (wide_in + down_blocks(hidden, w_downs[section_index])).astype(jnp.bfloat16)
    incoming = loss_grad.reshape(-1, D)
    gate_list, up_list, down_list, gain_list = ([], [], [], [])
    for section_index in reversed(range(N_SECTION)):
        wide_in = stored[section_index].astype(jnp.float32)
        unit_rows, row_scale, normed = norm_rows(wide_in, gains[section_index])
        gate_pre = jnp.dot(normed, w_gates[section_index], preferred_element_type=jnp.float32)
        up_pre = jnp.dot(normed, w_ups[section_index], preferred_element_type=jnp.float32)
        sig_gate = jax.nn.sigmoid(gate_pre)
        silu_gate = gate_pre * sig_gate
        hidden = (silu_gate * up_pre).astype(jnp.bfloat16)
        d_hidden = jnp.dot(incoming, w_downs[section_index].T, preferred_element_type=jnp.float32)
        d_gate_pre = (d_hidden * up_pre * sig_gate * (1.0 + gate_pre * (1.0 - sig_gate))).astype(jnp.bfloat16)
        d_up_pre = (d_hidden * silu_gate).astype(jnp.bfloat16)
        gate_list.append(jnp.dot(normed.T, d_gate_pre, preferred_element_type=jnp.float32))
        up_list.append(jnp.dot(normed.T, d_up_pre, preferred_element_type=jnp.float32))
        down_list.append(jnp.dot(hidden.T, incoming, preferred_element_type=jnp.float32))
        d_norm = input_blocks(d_gate_pre, d_up_pre, w_gates[section_index], w_ups[section_index])
        gain_list.append(lax.optimization_barrier(jnp.sum(d_norm * unit_rows, axis=0)))
        d_unit = d_norm * gains[section_index]
        incoming = (incoming.astype(jnp.float32) + row_scale * (d_unit - unit_rows * lax.optimization_barrier(jnp.mean(d_unit * unit_rows, axis=-1, keepdims=True)))).astype(jnp.bfloat16)
    return (jnp.stack(gate_list[::-1]), jnp.stack(up_list[::-1]), jnp.stack(down_list[::-1]), jnp.stack(gain_list[::-1]))

def reference(inputs, out_grad, local_gate, local_up, local_down, local_gain, anchor_gate, anchor_up, anchor_down, anchor_gain):
    site_sums = None
    for site_index in range(N_SITE):
        site_grads = site_gradients(inputs[site_index], out_grad[site_index], local_gate[site_index], local_up[site_index], local_down[site_index], local_gain[site_index])
        terms_now = (site_grads[0] + prox_weight * (local_gate[site_index].astype(jnp.float32) - anchor_gate.astype(jnp.float32)), site_grads[1] + prox_weight * (local_up[site_index].astype(jnp.float32) - anchor_up.astype(jnp.float32)), site_grads[2] + prox_weight * (local_down[site_index].astype(jnp.float32) - anchor_down.astype(jnp.float32)), site_grads[3] + prox_weight * (local_gain[site_index] - anchor_gain))
        if site_sums is None:
            site_sums = terms_now
        else:
            site_sums = tuple((left_side + right_side for left_side, right_side in zip(site_sums, terms_now)))
    return (site_sums[0] / N_SITE, site_sums[1] / N_SITE, site_sums[2] / N_SITE, site_sums[3] / N_SITE)
```

```python
import jax
import jax.numpy as jnp
from jax import lax
from jax.sharding import PartitionSpec as P

epsilon = 1e-06
prox_weight = 1.0


def passed_along(block, axis, distance):
    devices = range(lax.axis_size(axis))
    route = [(i - distance, i) for i in devices if i - distance in devices]
    return lax.ppermute(block, axis, route)


def norm_rows(wide_rows, gain_row):
    row_scale = lax.rsqrt(jnp.mean(wide_rows * wide_rows, axis=-1, keepdims=True) + epsilon)
    unit_rows = wide_rows * row_scale
    return (unit_rows, row_scale, (unit_rows * gain_row).astype(jnp.bfloat16))


def contract_rows(left_side, right_side):
    return lax.dot_general(
        left_side, right_side, (((0,), (0,)), ((), ())), preferred_element_type=jnp.float32
    )


def contract_cols(left_side, right_side):
    return lax.dot_general(
        left_side, right_side, (((1,), (1,)), ((), ())), preferred_element_type=jnp.float32
    )


def pick_block(blocks, block_index):
    return lax.dynamic_index_in_dim(blocks, block_index, 0, keepdims=False)


def gather_rows(chunks, tensor_count):
    n, c, d = chunks.shape
    spread = jnp.broadcast_to(chunks[:, None], (n, tensor_count, c, d))
    got = lax.all_to_all(spread, "tensor", 1, 1, tiled=False)
    return got.reshape(n, tensor_count * c, d)


def scatter_rows(parts, tensor_count):
    n, r, d = parts.shape
    split = parts.reshape(n, tensor_count, r // tensor_count, d)
    got = lax.all_to_all(split, "tensor", 1, 1, tiled=False)
    return jnp.sum(got.astype(jnp.float32), axis=1)


def shards(
    inputs,
    out_grad,
    local_gate,
    local_up,
    local_down,
    local_gain,
    anchor_gate,
    anchor_up,
    anchor_down,
    anchor_gain,
):
    w_gate = local_gate[0, 0]
    w_up = local_up[0, 0]
    w_down = local_down[0, 0]
    gain_row = local_gain[0, 0]
    site_feed = inputs[0]
    loss_grad = out_grad[0]
    micro_count = site_feed.shape[0]
    row_count = site_feed.shape[1]
    feature_count = site_feed.shape[2]
    section_count = lax.axis_size("section")
    section_index = lax.axis_index("section")
    tensor_count = lax.axis_size("tensor")
    tensor_index = lax.axis_index("tensor")
    site_count = lax.axis_size("site")
    chunk = row_count // tensor_count
    row_start = tensor_index * chunk
    back_lag = 2 * (section_count - 1)
    tick_count = micro_count + back_lag
    last_fwd_tick = micro_count + section_count - 3
    first_bwd_tick = section_count - 1

    def my_rows(rows):
        return lax.dynamic_slice_in_dim(rows, row_start, chunk, axis=0)

    def hidden_of(normed):
        gate_pre = jnp.dot(normed, w_gate, preferred_element_type=jnp.float32)
        up_pre = jnp.dot(normed, w_up, preferred_element_type=jnp.float32)
        return (gate_pre, up_pre, jax.nn.sigmoid(gate_pre))

    def slot_of(micro_index):
        is_valid = (micro_index >= 0) & (micro_index < micro_count)
        return (is_valid, jnp.clip(micro_index, 0, micro_count - 1))

    weight_grads = (
        jnp.zeros(w_gate.shape, jnp.float32),
        jnp.zeros(w_up.shape, jnp.float32),
        jnp.zeros(w_down.shape, jnp.float32),
    )
    gain_grad = jnp.zeros((feature_count,), jnp.float32)
    stored = jnp.zeros((micro_count, row_count, feature_count), jnp.bfloat16)
    recv_fwd = jnp.zeros((chunk, feature_count), jnp.bfloat16)
    recv_bwd = jnp.zeros((chunk, feature_count), jnp.bfloat16)
    for moment in range(tick_count):
        do_fwd = moment <= last_fwd_tick + 1
        do_bwd = moment >= first_bwd_tick
        fwd_valid, fwd_slot = slot_of(moment - section_index)
        bwd_valid, bwd_slot = slot_of(moment - back_lag + section_index)
        pieces = []
        if do_fwd:
            if moment < micro_count:
                fwd_chunk = jnp.where(section_index == 0, my_rows(site_feed[moment]), recv_fwd)
            else:
                fwd_chunk = recv_fwd
            pieces.append(fwd_chunk)
        if do_bwd:
            own_grad = my_rows(pick_block(loss_grad, bwd_slot))
            bwd_chunk = jnp.where(section_index == section_count - 1, own_grad, recv_bwd)
            bwd_chunk = jnp.where(bwd_valid, bwd_chunk, jnp.zeros_like(bwd_chunk))
            pieces.append(bwd_chunk)
        if moment == 0:
            gathered = [site_feed[0]]
        else:
            gathered_all = gather_rows(jnp.stack(pieces), tensor_count)
            gathered = [gathered_all[i] for i in range(len(pieces))]
        parts = []
        if do_fwd:
            fwd_rows = gathered[0]
            previous = pick_block(stored, fwd_slot)
            stored = lax.dynamic_update_index_in_dim(
                stored, jnp.where(fwd_valid, fwd_rows, previous), fwd_slot, 0
            )
        if do_fwd and moment <= last_fwd_tick:
            wide_in = fwd_rows.astype(jnp.float32)
            unit_rows, row_scale, normed = norm_rows(wide_in, gain_row)
            make_gate_pre, make_up_pre, make_sig_gate = hidden_of(normed)
            partial_value = jnp.dot(
                (make_gate_pre * make_sig_gate * make_up_pre).astype(jnp.bfloat16),
                w_down,
                preferred_element_type=jnp.float32,
            )
            parts.append(partial_value.astype(jnp.bfloat16))
        if do_bwd:
            incoming = gathered[-1]
            wide_in = pick_block(stored, bwd_slot).astype(jnp.float32)
            unit_rows, row_scale, normed = norm_rows(wide_in, gain_row)
            local_gate_pre, local_up_pre, sig_gate = hidden_of(normed)
            silu_gate = local_gate_pre * sig_gate
            hidden = (silu_gate * local_up_pre).astype(jnp.bfloat16)
            d_hidden = contract_cols(incoming, w_down)
            d_gate_pre = (
                d_hidden * local_up_pre * sig_gate * (1.0 + local_gate_pre * (1.0 - sig_gate))
            ).astype(jnp.bfloat16)
            d_up_pre = (d_hidden * silu_gate).astype(jnp.bfloat16)
            weight_grads = (
                weight_grads[0] + contract_rows(normed, d_gate_pre),
                weight_grads[1] + contract_rows(normed, d_up_pre),
                weight_grads[2] + contract_rows(hidden, incoming),
            )
            d_part = contract_cols(d_gate_pre, w_gate) + contract_cols(d_up_pre, w_up)
            parts.append(d_part.astype(jnp.bfloat16))
        if not parts:
            continue
        reduced = scatter_rows(jnp.stack(parts), tensor_count)
        if do_fwd and moment <= last_fwd_tick:
            out_chunk = (fwd_chunk.astype(jnp.float32) + reduced[0]).astype(jnp.bfloat16)
            recv_fwd = passed_along(out_chunk, "section", 1)
        if do_bwd:
            d_norm = reduced[-1]
            unit_mine = my_rows(unit_rows)
            scale_mine = my_rows(row_scale)
            gain_grad = gain_grad + jnp.sum(d_norm * unit_mine, axis=0)
            if moment + 1 < tick_count:
                d_unit = d_norm * gain_row
                sent_back = (
                    bwd_chunk.astype(jnp.float32)
                    + scale_mine
                    * (d_unit - unit_mine * jnp.mean(d_unit * unit_mine, axis=-1, keepdims=True))
                ).astype(jnp.bfloat16)
                recv_bwd = passed_along(sent_back, "section", -1)
    gain_term = gain_grad + jnp.where(
        tensor_index == 0, prox_weight * (gain_row - anchor_gain[0]), jnp.zeros_like(gain_row)
    )
    gate_term = weight_grads[0] + prox_weight * (
        w_gate.astype(jnp.float32) - anchor_gate[0].astype(jnp.float32)
    )
    up_term = weight_grads[1] + prox_weight * (
        w_up.astype(jnp.float32) - anchor_up[0].astype(jnp.float32)
    )
    down_term = weight_grads[2] + prox_weight * (
        w_down.astype(jnp.float32) - anchor_down[0].astype(jnp.float32)
    )
    gate_total, up_total, down_total = (
        lax.psum(gate_term.astype(jnp.bfloat16), "site").astype(jnp.float32),
        lax.psum(up_term.astype(jnp.bfloat16), "site").astype(jnp.float32),
        lax.psum(down_term.astype(jnp.bfloat16), "site").astype(jnp.float32),
    )
    gain_total = lax.psum(gain_term, ("site", "tensor"))
    return (
        (gate_total / site_count)[None],
        (up_total / site_count)[None],
        (down_total / site_count)[None],
        (gain_total / site_count)[None],
    )


def solution(mesh):
    in_specs = (
        P("site", None, None, None),
        P("site", None, None, None),
        P("site", "section", None, "tensor"),
        P("site", "section", None, "tensor"),
        P("site", "section", "tensor", None),
        P("site", "section", None),
        P("section", None, "tensor"),
        P("section", None, "tensor"),
        P("section", "tensor", None),
        P("section", None),
    )
    out_specs = (
        P("section", None, "tensor"),
        P("section", None, "tensor"),
        P("section", "tensor", None),
        P("section", None),
    )
    return jax.shard_map(shards, mesh=mesh, in_specs=in_specs, out_specs=out_specs, check_vma=False)
```

```python
import jax
import jax.numpy as jnp
from jax import lax
from jax.sharding import PartitionSpec as P

epsilon = 1e-06
prox_weight = 1.0


def passed_along(block, axis, distance):
    devices = range(lax.axis_size(axis))
    route = [(i - distance, i) for i in devices if i - distance in devices]
    return lax.ppermute(block, axis, route)


def norm_rows(wide_rows, gain_row):
    row_scale = lax.rsqrt(jnp.mean(wide_rows * wide_rows, axis=-1, keepdims=True) + epsilon)
    unit_rows = wide_rows * row_scale
    return (unit_rows, row_scale, (unit_rows * gain_row).astype(jnp.bfloat16))


def contract_rows(left_side, right_side):
    return lax.dot_general(
        left_side, right_side, (((0,), (0,)), ((), ())), preferred_element_type=jnp.float32
    )


def contract_cols(left_side, right_side):
    return lax.dot_general(
        left_side, right_side, (((1,), (1,)), ((), ())), preferred_element_type=jnp.float32
    )


def pick_block(blocks, block_index):
    return lax.dynamic_index_in_dim(blocks, block_index, 0, keepdims=False)


def gather_rows(chunks, tensor_count):
    n, c, d = chunks.shape
    spread = jnp.broadcast_to(chunks[:, None], (n, tensor_count, c, d))
    got = lax.all_to_all(spread, "tensor", 1, 1, tiled=False)
    return got.reshape(n, tensor_count * c, d)


def scatter_rows(parts, tensor_count):
    n, r, d = parts.shape
    split = parts.reshape(n, tensor_count, r // tensor_count, d)
    got = lax.all_to_all(split, "tensor", 1, 1, tiled=False)
    return jnp.sum(got.astype(jnp.float32), axis=1)


def shards(
    inputs,
    out_grad,
    local_gate,
    local_up,
    local_down,
    local_gain,
    anchor_gate,
    anchor_up,
    anchor_down,
    anchor_gain,
):
    w_gate = local_gate[0, 0]
    w_up = local_up[0, 0]
    w_down = local_down[0, 0]
    gain_row = local_gain[0, 0]
    site_feed = inputs[0]
    loss_grad = out_grad[0]
    micro_count = site_feed.shape[0]
    row_count = site_feed.shape[1]
    feature_count = site_feed.shape[2]
    section_count = lax.axis_size("section")
    section_index = lax.axis_index("section")
    tensor_count = lax.axis_size("tensor")
    tensor_index = lax.axis_index("tensor")
    site_count = lax.axis_size("site")
    chunk = row_count // tensor_count
    row_start = tensor_index * chunk
    back_lag = 2 * (section_count - 1)
    tick_count = micro_count + back_lag
    last_fwd_tick = micro_count + section_count - 3
    first_bwd_tick = section_count - 1

    def my_rows(rows):
        return lax.dynamic_slice_in_dim(rows, row_start, chunk, axis=0)

    def hidden_of(normed):
        gate_pre = jnp.dot(normed, w_gate, preferred_element_type=jnp.float32)
        up_pre = jnp.dot(normed, w_up, preferred_element_type=jnp.float32)
        return (gate_pre, up_pre, jax.nn.sigmoid(gate_pre))

    def slot_of(micro_index):
        is_valid = (micro_index >= 0) & (micro_index < micro_count)
        return (is_valid, jnp.clip(micro_index, 0, micro_count - 1))

    weight_grads = (
        jnp.zeros(w_gate.shape, jnp.float32),
        jnp.zeros(w_up.shape, jnp.float32),
        jnp.zeros(w_down.shape, jnp.float32),
    )
    hidden_count = w_gate.shape[1]
    gain_grad = jnp.zeros((feature_count,), jnp.float32)
    slots = micro_count + 1
    stored_chunk = jnp.zeros((slots, chunk, feature_count), jnp.bfloat16)
    stored_normed = jnp.zeros((slots, row_count, feature_count), jnp.bfloat16)
    stored_gate = jnp.zeros((slots, row_count, hidden_count), jnp.float32)
    stored_up = jnp.zeros((slots, row_count, hidden_count), jnp.float32)
    recv_fwd = jnp.zeros((chunk, feature_count), jnp.bfloat16)
    recv_bwd = jnp.zeros((chunk, feature_count), jnp.bfloat16)

    def keep(stack, value, slot):
        return lax.dynamic_update_index_in_dim(stack, value, slot, 0)

    for moment in range(tick_count):
        do_fwd = moment <= last_fwd_tick + 1
        do_bwd = moment >= first_bwd_tick
        fwd_valid, fwd_slot = slot_of(moment - section_index)
        fwd_slot = jnp.where(fwd_valid, fwd_slot, micro_count)
        bwd_valid, bwd_slot = slot_of(moment - back_lag + section_index)
        pieces = []
        if do_fwd:
            if moment < micro_count:
                fwd_chunk = jnp.where(section_index == 0, my_rows(site_feed[moment]), recv_fwd)
            else:
                fwd_chunk = recv_fwd
            pieces.append(fwd_chunk)
        if do_bwd:
            own_grad = my_rows(pick_block(loss_grad, bwd_slot))
            bwd_chunk = jnp.where(section_index == section_count - 1, own_grad, recv_bwd)
            bwd_chunk = jnp.where(bwd_valid, bwd_chunk, jnp.zeros_like(bwd_chunk))
            pieces.append(bwd_chunk)
        if moment == 0:
            gathered = [site_feed[0]]
        else:
            gathered_all = gather_rows(jnp.stack(pieces), tensor_count)
            gathered = [gathered_all[i] for i in range(len(pieces))]
        parts = []
        if do_fwd:
            wide_in = gathered[0].astype(jnp.float32)
            unit_rows, row_scale, normed = norm_rows(wide_in, gain_row)
            make_gate_pre, make_up_pre, make_sig_gate = hidden_of(normed)
            stored_chunk = keep(stored_chunk, fwd_chunk, fwd_slot)
            stored_normed = keep(stored_normed, normed, fwd_slot)
            stored_gate = keep(stored_gate, make_gate_pre, fwd_slot)
            stored_up = keep(stored_up, make_up_pre, fwd_slot)
        if do_fwd and moment <= last_fwd_tick:
            partial_value = jnp.dot(
                (make_gate_pre * make_sig_gate * make_up_pre).astype(jnp.bfloat16),
                w_down,
                preferred_element_type=jnp.float32,
            )
            parts.append(partial_value.astype(jnp.bfloat16))
        if do_bwd:
            incoming = gathered[-1]
            normed = pick_block(stored_normed, bwd_slot)
            local_gate_pre = pick_block(stored_gate, bwd_slot)
            local_up_pre = pick_block(stored_up, bwd_slot)
            sig_gate = jax.nn.sigmoid(local_gate_pre)
            silu_gate = local_gate_pre * sig_gate
            hidden = (silu_gate * local_up_pre).astype(jnp.bfloat16)
            d_hidden = contract_cols(incoming, w_down)
            d_gate_pre = (
                d_hidden * local_up_pre * sig_gate * (1.0 + local_gate_pre * (1.0 - sig_gate))
            ).astype(jnp.bfloat16)
            d_up_pre = (d_hidden * silu_gate).astype(jnp.bfloat16)
            weight_grads = (
                weight_grads[0] + contract_rows(normed, d_gate_pre),
                weight_grads[1] + contract_rows(normed, d_up_pre),
                weight_grads[2] + contract_rows(hidden, incoming),
            )
            d_part = contract_cols(d_gate_pre, w_gate) + contract_cols(d_up_pre, w_up)
            parts.append(d_part.astype(jnp.bfloat16))
        reduced = scatter_rows(jnp.stack(parts), tensor_count)
        if do_fwd and moment <= last_fwd_tick:
            out_chunk = (fwd_chunk.astype(jnp.float32) + reduced[0]).astype(jnp.bfloat16)
            recv_fwd = passed_along(out_chunk, "section", 1)
        if do_bwd:
            d_norm = reduced[-1]
            unit_mine, scale_mine, _ = norm_rows(
                pick_block(stored_chunk, bwd_slot).astype(jnp.float32), gain_row
            )
            gain_grad = gain_grad + jnp.sum(d_norm * unit_mine, axis=0)
            if moment + 1 < tick_count:
                d_unit = d_norm * gain_row
                sent_back = (
                    bwd_chunk.astype(jnp.float32)
                    + scale_mine
                    * (d_unit - unit_mine * jnp.mean(d_unit * unit_mine, axis=-1, keepdims=True))
                ).astype(jnp.bfloat16)
                recv_bwd = passed_along(sent_back, "section", -1)
    gain_term = gain_grad + jnp.where(
        tensor_index == 0, prox_weight * (gain_row - anchor_gain[0]), jnp.zeros_like(gain_row)
    )
    gate_term = weight_grads[0] + prox_weight * (
        w_gate.astype(jnp.float32) - anchor_gate[0].astype(jnp.float32)
    )
    up_term = weight_grads[1] + prox_weight * (
        w_up.astype(jnp.float32) - anchor_up[0].astype(jnp.float32)
    )
    down_term = weight_grads[2] + prox_weight * (
        w_down.astype(jnp.float32) - anchor_down[0].astype(jnp.float32)
    )
    gate_total, up_total, down_total = (
        lax.psum(gate_term.astype(jnp.bfloat16), "site").astype(jnp.float32),
        lax.psum(up_term.astype(jnp.bfloat16), "site").astype(jnp.float32),
        lax.psum(down_term.astype(jnp.bfloat16), "site").astype(jnp.float32),
    )
    group_count = site_count * tensor_count
    gain_spread = jnp.broadcast_to(gain_term[None], (group_count, feature_count))
    gain_total = jnp.sum(lax.all_to_all(gain_spread, ("site", "tensor"), 0, 0, tiled=False), axis=0)
    return (
        (gate_total / site_count)[None],
        (up_total / site_count)[None],
        (down_total / site_count)[None],
        (gain_total / site_count)[None],
    )


def solution(mesh):
    in_specs = (
        P("site", None, None, None),
        P("site", None, None, None),
        P("site", "section", None, "tensor"),
        P("site", "section", None, "tensor"),
        P("site", "section", "tensor", None),
        P("site", "section", None),
        P("section", None, "tensor"),
        P("section", None, "tensor"),
        P("section", "tensor", None),
        P("section", None),
    )
    out_specs = (
        P("section", None, "tensor"),
        P("section", None, "tensor"),
        P("section", "tensor", None),
        P("section", None),
    )
    return jax.shard_map(shards, mesh=mesh, in_specs=in_specs, out_specs=out_specs, check_vma=False)
```

```python
import jax
import jax.numpy as jnp
from jax import lax
from jax.sharding import PartitionSpec as P

epsilon = 1e-06
prox_weight = 1.0


def passed_along(block, axis, distance):
    devices = range(lax.axis_size(axis))
    route = [(i - distance, i) for i in devices if i - distance in devices]
    return lax.ppermute(block, axis, route)


def norm_rows(wide_rows, gain_row):
    row_scale = lax.rsqrt(jnp.mean(wide_rows * wide_rows, axis=-1, keepdims=True) + epsilon)
    unit_rows = wide_rows * row_scale
    return (unit_rows, row_scale, (unit_rows * gain_row).astype(jnp.bfloat16))


def contract_rows(left_side, right_side):
    return lax.dot_general(
        left_side, right_side, (((0,), (0,)), ((), ())), preferred_element_type=jnp.float32
    )


def contract_cols(left_side, right_side):
    return lax.dot_general(
        left_side, right_side, (((1,), (1,)), ((), ())), preferred_element_type=jnp.float32
    )


def pick_block(blocks, block_index):
    return lax.dynamic_index_in_dim(blocks, block_index, 0, keepdims=False)


def gather_rows(chunks, tensor_count):
    n, c, d = chunks.shape
    spread = jnp.broadcast_to(chunks[:, None], (n, tensor_count, c, d))
    got = lax.all_to_all(spread, "tensor", 1, 1, tiled=False)
    return got.reshape(n, tensor_count * c, d)


def scatter_rows(parts, tensor_count):
    n, r, d = parts.shape
    split = parts.reshape(n, tensor_count, r // tensor_count, d)
    got = lax.all_to_all(split, "tensor", 1, 1, tiled=False)
    return jnp.sum(got.astype(jnp.float32), axis=1)


def swap_sites(block, flip):
    return lax.ppermute(block, "site", [(i, i ^ flip) for i in range(lax.axis_size("site"))])


def halving_site_sum(wide):
    site_index = lax.axis_index("site")
    core_bit = site_index % 2
    chip_bit = site_index // 2
    half = wide.shape[0] // 2
    quarter = half // 2
    sent = lax.dynamic_slice_in_dim(wide, (1 - core_bit) * half, half).astype(jnp.bfloat16)
    kept = lax.dynamic_slice_in_dim(wide, core_bit * half, half)
    pair_sum = kept + swap_sites(sent, 1).astype(jnp.float32)
    sent = lax.dynamic_slice_in_dim(pair_sum, (1 - chip_bit) * quarter, quarter).astype(jnp.bfloat16)
    kept = lax.dynamic_slice_in_dim(pair_sum, chip_bit * quarter, quarter)
    own = (kept + swap_sites(sent, 2).astype(jnp.float32)).astype(jnp.bfloat16)
    other = swap_sites(own, 2)
    own = jnp.where(chip_bit == 0, jnp.concatenate([own, other]), jnp.concatenate([other, own]))
    other = swap_sites(own, 1)
    whole = jnp.where(core_bit == 0, jnp.concatenate([own, other]), jnp.concatenate([other, own]))
    return whole.astype(jnp.float32)


def shards(
    inputs,
    out_grad,
    local_gate,
    local_up,
    local_down,
    local_gain,
    anchor_gate,
    anchor_up,
    anchor_down,
    anchor_gain,
):
    w_gate = local_gate[0, 0]
    w_up = local_up[0, 0]
    w_down = local_down[0, 0]
    gain_row = local_gain[0, 0]
    site_feed = inputs[0]
    loss_grad = out_grad[0]
    micro_count = site_feed.shape[0]
    row_count = site_feed.shape[1]
    feature_count = site_feed.shape[2]
    section_count = lax.axis_size("section")
    section_index = lax.axis_index("section")
    tensor_count = lax.axis_size("tensor")
    tensor_index = lax.axis_index("tensor")
    site_count = lax.axis_size("site")
    chunk = row_count // tensor_count
    row_start = tensor_index * chunk
    back_lag = 2 * (section_count - 1)
    tick_count = micro_count + back_lag
    last_fwd_tick = micro_count + section_count - 3
    first_bwd_tick = section_count - 1

    def my_rows(rows):
        return lax.dynamic_slice_in_dim(rows, row_start, chunk, axis=0)

    def hidden_of(normed):
        gate_pre = jnp.dot(normed, w_gate, preferred_element_type=jnp.float32)
        up_pre = jnp.dot(normed, w_up, preferred_element_type=jnp.float32)
        return (gate_pre, up_pre, jax.nn.sigmoid(gate_pre))

    def slot_of(micro_index):
        is_valid = (micro_index >= 0) & (micro_index < micro_count)
        return (is_valid, jnp.clip(micro_index, 0, micro_count - 1))

    weight_grads = (
        jnp.zeros(w_gate.shape, jnp.float32),
        jnp.zeros(w_up.shape, jnp.float32),
        jnp.zeros(w_down.shape, jnp.float32),
    )
    hidden_count = w_gate.shape[1]
    gain_grad = jnp.zeros((feature_count,), jnp.float32)
    slots = micro_count + 1
    stored_chunk = jnp.zeros((slots, chunk, feature_count), jnp.bfloat16)
    stored_normed = jnp.zeros((slots, row_count, feature_count), jnp.bfloat16)
    stored_gate = jnp.zeros((slots, row_count, hidden_count), jnp.float32)
    stored_up = jnp.zeros((slots, row_count, hidden_count), jnp.float32)
    recv_fwd = jnp.zeros((chunk, feature_count), jnp.bfloat16)
    recv_bwd = jnp.zeros((chunk, feature_count), jnp.bfloat16)

    def keep(stack, value, slot):
        return lax.dynamic_update_index_in_dim(stack, value, slot, 0)

    for moment in range(tick_count):
        do_fwd = moment <= last_fwd_tick + 1
        do_bwd = moment >= first_bwd_tick
        fwd_valid, fwd_slot = slot_of(moment - section_index)
        fwd_slot = jnp.where(fwd_valid, fwd_slot, micro_count)
        bwd_valid, bwd_slot = slot_of(moment - back_lag + section_index)
        pieces = []
        if do_fwd:
            if moment < micro_count:
                fwd_chunk = jnp.where(section_index == 0, my_rows(site_feed[moment]), recv_fwd)
            else:
                fwd_chunk = recv_fwd
            pieces.append(fwd_chunk)
        if do_bwd:
            own_grad = my_rows(pick_block(loss_grad, bwd_slot))
            bwd_chunk = jnp.where(section_index == section_count - 1, own_grad, recv_bwd)
            bwd_chunk = jnp.where(bwd_valid, bwd_chunk, jnp.zeros_like(bwd_chunk))
            pieces.append(bwd_chunk)
        if moment == 0:
            gathered = [site_feed[0]]
        else:
            gathered_all = gather_rows(jnp.stack(pieces), tensor_count)
            gathered = [gathered_all[i] for i in range(len(pieces))]
        parts = []
        if do_fwd:
            wide_in = gathered[0].astype(jnp.float32)
            unit_rows, row_scale, normed = norm_rows(wide_in, gain_row)
            make_gate_pre, make_up_pre, make_sig_gate = hidden_of(normed)
            stored_chunk = keep(stored_chunk, fwd_chunk, fwd_slot)
            stored_normed = keep(stored_normed, normed, fwd_slot)
            stored_gate = keep(stored_gate, make_gate_pre, fwd_slot)
            stored_up = keep(stored_up, make_up_pre, fwd_slot)
        if do_fwd and moment <= last_fwd_tick:
            partial_value = jnp.dot(
                (make_gate_pre * make_sig_gate * make_up_pre).astype(jnp.bfloat16),
                w_down,
                preferred_element_type=jnp.float32,
            )
            parts.append(partial_value.astype(jnp.bfloat16))
        if do_bwd:
            incoming = gathered[-1]
            normed = pick_block(stored_normed, bwd_slot)
            local_gate_pre = pick_block(stored_gate, bwd_slot)
            local_up_pre = pick_block(stored_up, bwd_slot)
            sig_gate = jax.nn.sigmoid(local_gate_pre)
            silu_gate = local_gate_pre * sig_gate
            hidden = (silu_gate * local_up_pre).astype(jnp.bfloat16)
            d_hidden = contract_cols(incoming, w_down)
            d_gate_pre = (
                d_hidden * local_up_pre * sig_gate * (1.0 + local_gate_pre * (1.0 - sig_gate))
            ).astype(jnp.bfloat16)
            d_up_pre = (d_hidden * silu_gate).astype(jnp.bfloat16)
            weight_grads = (
                weight_grads[0] + contract_rows(normed, d_gate_pre),
                weight_grads[1] + contract_rows(normed, d_up_pre),
                weight_grads[2] + contract_rows(hidden, incoming),
            )
            d_part = contract_cols(d_gate_pre, w_gate) + contract_cols(d_up_pre, w_up)
            parts.append(d_part.astype(jnp.bfloat16))
        reduced = scatter_rows(jnp.stack(parts), tensor_count)
        if do_fwd and moment <= last_fwd_tick:
            out_chunk = (fwd_chunk.astype(jnp.float32) + reduced[0]).astype(jnp.bfloat16)
            recv_fwd = passed_along(out_chunk, "section", 1)
        if do_bwd:
            d_norm = reduced[-1]
            unit_mine, scale_mine, _ = norm_rows(
                pick_block(stored_chunk, bwd_slot).astype(jnp.float32), gain_row
            )
            gain_grad = gain_grad + jnp.sum(d_norm * unit_mine, axis=0)
            if moment + 1 < tick_count:
                d_unit = d_norm * gain_row
                sent_back = (
                    bwd_chunk.astype(jnp.float32)
                    + scale_mine
                    * (d_unit - unit_mine * jnp.mean(d_unit * unit_mine, axis=-1, keepdims=True))
                ).astype(jnp.bfloat16)
                recv_bwd = passed_along(sent_back, "section", -1)
    gain_term = gain_grad + jnp.where(
        tensor_index == 0, prox_weight * (gain_row - anchor_gain[0]), jnp.zeros_like(gain_row)
    )
    gate_term = weight_grads[0] + prox_weight * (
        w_gate.astype(jnp.float32) - anchor_gate[0].astype(jnp.float32)
    )
    up_term = weight_grads[1] + prox_weight * (
        w_up.astype(jnp.float32) - anchor_up[0].astype(jnp.float32)
    )
    down_term = weight_grads[2] + prox_weight * (
        w_down.astype(jnp.float32) - anchor_down[0].astype(jnp.float32)
    )
    gate_total, up_total, down_total = (
        lax.psum(gate_term.astype(jnp.bfloat16), "site").astype(jnp.float32),
        lax.psum(up_term.astype(jnp.bfloat16), "site").astype(jnp.float32),
        halving_site_sum(down_term),
    )
    group_count = site_count * tensor_count
    gain_spread = jnp.broadcast_to(gain_term[None], (group_count, feature_count))
    gain_total = jnp.sum(lax.all_to_all(gain_spread, ("site", "tensor"), 0, 0, tiled=False), axis=0)
    return (
        (gate_total / site_count)[None],
        (up_total / site_count)[None],
        (down_total / site_count)[None],
        (gain_total / site_count)[None],
    )


def solution(mesh):
    in_specs = (
        P("site", None, None, None),
        P("site", None, None, None),
        P("site", "section", None, "tensor"),
        P("site", "section", None, "tensor"),
        P("site", "section", "tensor", None),
        P("site", "section", None),
        P("section", None, "tensor"),
        P("section", None, "tensor"),
        P("section", "tensor", None),
        P("section", None),
    )
    out_specs = (
        P("section", None, "tensor"),
        P("section", None, "tensor"),
        P("section", "tensor", None),
        P("section", None),
    )
    return jax.shard_map(shards, mesh=mesh, in_specs=in_specs, out_specs=out_specs, check_vma=False)
```

```python
import jax
import jax.numpy as jnp
from jax import lax
from jax.sharding import PartitionSpec as P

epsilon = 1e-06
prox_weight = 1.0


def passed_along(block, axis, distance):
    devices = range(lax.axis_size(axis))
    route = [(i - distance, i) for i in devices if i - distance in devices]
    return lax.ppermute(block, axis, route)


def norm_rows(wide_rows, gain_row):
    row_scale = lax.rsqrt(jnp.mean(wide_rows * wide_rows, axis=-1, keepdims=True) + epsilon)
    unit_rows = wide_rows * row_scale
    return (unit_rows, row_scale, (unit_rows * gain_row).astype(jnp.bfloat16))


def contract_rows(left_side, right_side):
    return lax.dot_general(
        left_side, right_side, (((0,), (0,)), ((), ())), preferred_element_type=jnp.float32
    )


def contract_cols(left_side, right_side):
    return lax.dot_general(
        left_side, right_side, (((1,), (1,)), ((), ())), preferred_element_type=jnp.float32
    )


def pick_block(blocks, block_index):
    return lax.dynamic_index_in_dim(blocks, block_index, 0, keepdims=False)


def gather_rows(chunks, tensor_count):
    n, c, d = chunks.shape
    spread = jnp.broadcast_to(chunks[:, None], (n, tensor_count, c, d))
    got = lax.all_to_all(spread, "tensor", 1, 1, tiled=False)
    return got.reshape(n, tensor_count * c, d)


def scatter_rows(parts, tensor_count):
    n, r, d = parts.shape
    split = parts.reshape(n, tensor_count, r // tensor_count, d)
    got = lax.all_to_all(split, "tensor", 1, 1, tiled=False)
    return jnp.sum(got.astype(jnp.float32), axis=1)


def swap_sites(block, flip):
    return lax.ppermute(block, "site", [(i, i ^ flip) for i in range(lax.axis_size("site"))])


def halving_site_sum(wide):
    site_index = lax.axis_index("site")
    core_bit = site_index % 2
    chip_bit = site_index // 2
    half = wide.shape[0] // 2
    quarter = half // 2
    sent = lax.dynamic_slice_in_dim(wide, (1 - core_bit) * half, half).astype(jnp.bfloat16)
    kept = lax.dynamic_slice_in_dim(wide, core_bit * half, half)
    pair_sum = kept + swap_sites(sent, 1).astype(jnp.float32)
    sent = lax.dynamic_slice_in_dim(pair_sum, (1 - chip_bit) * quarter, quarter).astype(jnp.bfloat16)
    kept = lax.dynamic_slice_in_dim(pair_sum, chip_bit * quarter, quarter)
    own = (kept + swap_sites(sent, 2).astype(jnp.float32)).astype(jnp.bfloat16)
    other = swap_sites(own, 2)
    own = jnp.where(chip_bit == 0, jnp.concatenate([own, other]), jnp.concatenate([other, own]))
    other = swap_sites(own, 1)
    whole = jnp.where(core_bit == 0, jnp.concatenate([own, other]), jnp.concatenate([other, own]))
    return whole.astype(jnp.float32)


def shards(
    inputs,
    out_grad,
    local_gate,
    local_up,
    local_down,
    local_gain,
    anchor_gate,
    anchor_up,
    anchor_down,
    anchor_gain,
):
    w_gate = local_gate[0, 0]
    w_up = local_up[0, 0]
    w_down = local_down[0, 0]
    gain_row = local_gain[0, 0]
    site_feed = inputs[0]
    loss_grad = out_grad[0]
    micro_count = site_feed.shape[0]
    row_count = site_feed.shape[1]
    feature_count = site_feed.shape[2]
    section_count = lax.axis_size("section")
    section_index = lax.axis_index("section")
    tensor_count = lax.axis_size("tensor")
    tensor_index = lax.axis_index("tensor")
    site_count = lax.axis_size("site")
    chunk = row_count // tensor_count
    row_start = tensor_index * chunk
    back_lag = 2 * (section_count - 1)
    tick_count = micro_count + back_lag
    last_fwd_tick = micro_count + section_count - 3
    first_bwd_tick = section_count - 1

    def my_rows(rows):
        return lax.dynamic_slice_in_dim(rows, row_start, chunk, axis=0)

    def hidden_of(normed):
        gate_pre = jnp.dot(normed, w_gate, preferred_element_type=jnp.float32)
        up_pre = jnp.dot(normed, w_up, preferred_element_type=jnp.float32)
        return (gate_pre, up_pre, jax.nn.sigmoid(gate_pre))

    def slot_of(micro_index):
        is_valid = (micro_index >= 0) & (micro_index < micro_count)
        return (is_valid, jnp.clip(micro_index, 0, micro_count - 1))

    weight_grads = (
        jnp.zeros(w_gate.shape, jnp.float32),
        jnp.zeros(w_up.shape, jnp.float32),
        jnp.zeros(w_down.shape, jnp.float32),
    )
    hidden_count = w_gate.shape[1]
    gain_grad = jnp.zeros((feature_count,), jnp.float32)
    slots = micro_count + 1
    stored_chunk = jnp.zeros((slots, chunk, feature_count), jnp.bfloat16)
    stored_normed = jnp.zeros((slots, row_count, feature_count), jnp.bfloat16)
    stored_gate = jnp.zeros((slots, row_count, hidden_count), jnp.float32)
    stored_up = jnp.zeros((slots, row_count, hidden_count), jnp.float32)
    recv_fwd = jnp.zeros((chunk, feature_count), jnp.bfloat16)
    recv_bwd = jnp.zeros((chunk, feature_count), jnp.bfloat16)

    def keep(stack, value, slot):
        return lax.dynamic_update_index_in_dim(stack, value, slot, 0)

    for moment in range(tick_count):
        do_fwd = moment <= last_fwd_tick + 1
        do_bwd = moment >= first_bwd_tick
        fwd_valid, fwd_slot = slot_of(moment - section_index)
        fwd_slot = jnp.where(fwd_valid, fwd_slot, micro_count)
        bwd_valid, bwd_slot = slot_of(moment - back_lag + section_index)
        pieces = []
        if do_fwd:
            if moment < micro_count:
                fwd_chunk = jnp.where(section_index == 0, my_rows(site_feed[moment]), recv_fwd)
            else:
                fwd_chunk = recv_fwd
            pieces.append(fwd_chunk)
        if do_bwd:
            own_grad = my_rows(pick_block(loss_grad, bwd_slot))
            bwd_chunk = jnp.where(section_index == section_count - 1, own_grad, recv_bwd)
            bwd_chunk = jnp.where(bwd_valid, bwd_chunk, jnp.zeros_like(bwd_chunk))
            pieces.append(bwd_chunk)
        if moment == 0:
            gathered = [site_feed[0]]
        else:
            gathered_all = gather_rows(jnp.stack(pieces), tensor_count)
            gathered = [gathered_all[i] for i in range(len(pieces))]
        parts = []
        if do_fwd:
            wide_in = gathered[0].astype(jnp.float32)
            unit_rows, row_scale, normed = norm_rows(wide_in, gain_row)
            make_gate_pre, make_up_pre, make_sig_gate = hidden_of(normed)
            stored_chunk = keep(stored_chunk, fwd_chunk, fwd_slot)
            stored_normed = keep(stored_normed, normed, fwd_slot)
            stored_gate = keep(stored_gate, make_gate_pre, fwd_slot)
            stored_up = keep(stored_up, make_up_pre, fwd_slot)
        if do_fwd and moment <= last_fwd_tick:
            partial_value = jnp.dot(
                (make_gate_pre * make_sig_gate * make_up_pre).astype(jnp.bfloat16),
                w_down,
                preferred_element_type=jnp.float32,
            )
            parts.append(partial_value.astype(jnp.bfloat16))
        if do_bwd:
            incoming = gathered[-1]
            normed = pick_block(stored_normed, bwd_slot)
            local_gate_pre = pick_block(stored_gate, bwd_slot)
            local_up_pre = pick_block(stored_up, bwd_slot)
            sig_gate = jax.nn.sigmoid(local_gate_pre)
            silu_gate = local_gate_pre * sig_gate
            hidden = (silu_gate * local_up_pre).astype(jnp.bfloat16)
            d_hidden = contract_cols(incoming, w_down)
            d_gate_pre = (
                d_hidden * local_up_pre * sig_gate * (1.0 + local_gate_pre * (1.0 - sig_gate))
            ).astype(jnp.bfloat16)
            d_up_pre = (d_hidden * silu_gate).astype(jnp.bfloat16)
            weight_grads = (
                weight_grads[0] + contract_rows(normed, d_gate_pre),
                weight_grads[1] + contract_rows(normed, d_up_pre),
                weight_grads[2] + contract_rows(hidden, incoming),
            )
            d_part = contract_cols(d_gate_pre, w_gate) + contract_cols(d_up_pre, w_up)
            parts.append(d_part.astype(jnp.bfloat16))
        reduced = scatter_rows(jnp.stack(parts), tensor_count)
        if do_fwd and moment <= last_fwd_tick:
            out_chunk = (fwd_chunk.astype(jnp.float32) + reduced[0]).astype(jnp.bfloat16)
            recv_fwd = passed_along(out_chunk, "section", 1)
        if do_bwd:
            d_norm = reduced[-1]
            unit_mine, scale_mine, _ = norm_rows(
                pick_block(stored_chunk, bwd_slot).astype(jnp.float32), gain_row
            )
            gain_grad = gain_grad + jnp.sum(d_norm * unit_mine, axis=0)
            if moment + 1 < tick_count:
                d_unit = d_norm * gain_row
                sent_back = (
                    bwd_chunk.astype(jnp.float32)
                    + scale_mine
                    * (d_unit - unit_mine * jnp.mean(d_unit * unit_mine, axis=-1, keepdims=True))
                ).astype(jnp.bfloat16)
                recv_bwd = passed_along(sent_back, "section", -1)
    gain_term = gain_grad + jnp.where(
        tensor_index == 0, prox_weight * (gain_row - anchor_gain[0]), jnp.zeros_like(gain_row)
    )
    gate_term = weight_grads[0] + prox_weight * (
        w_gate.astype(jnp.float32) - anchor_gate[0].astype(jnp.float32)
    )
    up_term = weight_grads[1] + prox_weight * (
        w_up.astype(jnp.float32) - anchor_up[0].astype(jnp.float32)
    )
    down_term = weight_grads[2] + prox_weight * (
        w_down.astype(jnp.float32) - anchor_down[0].astype(jnp.float32)
    )
    gate_total, up_total, down_total = (
        halving_site_sum(gate_term),
        halving_site_sum(up_term),
        halving_site_sum(down_term),
    )
    group_count = site_count * tensor_count
    gain_spread = jnp.broadcast_to(gain_term[None], (group_count, feature_count))
    gain_total = jnp.sum(lax.all_to_all(gain_spread, ("site", "tensor"), 0, 0, tiled=False), axis=0)
    return (
        (gate_total / site_count)[None],
        (up_total / site_count)[None],
        (down_total / site_count)[None],
        (gain_total / site_count)[None],
    )


def solution(mesh):
    in_specs = (
        P("site", None, None, None),
        P("site", None, None, None),
        P("site", "section", None, "tensor"),
        P("site", "section", None, "tensor"),
        P("site", "section", "tensor", None),
        P("site", "section", None),
        P("section", None, "tensor"),
        P("section", None, "tensor"),
        P("section", "tensor", None),
        P("section", None),
    )
    out_specs = (
        P("section", None, "tensor"),
        P("section", None, "tensor"),
        P("section", "tensor", None),
        P("section", None),
    )
    return jax.shard_map(shards, mesh=mesh, in_specs=in_specs, out_specs=out_specs, check_vma=False)
```

```python
import jax
import jax.numpy as jnp
from jax import lax
from jax.sharding import PartitionSpec as P

epsilon = 1e-06
prox_weight = 1.0


def passed_along(block, axis, distance):
    devices = range(lax.axis_size(axis))
    route = [(i - distance, i) for i in devices if i - distance in devices]
    return lax.ppermute(block, axis, route)


def norm_rows(wide_rows, gain_row):
    row_scale = lax.rsqrt(jnp.mean(wide_rows * wide_rows, axis=-1, keepdims=True) + epsilon)
    unit_rows = wide_rows * row_scale
    return (unit_rows, row_scale, (unit_rows * gain_row).astype(jnp.bfloat16))


def contract_rows(left_side, right_side):
    return lax.dot_general(
        left_side, right_side, (((0,), (0,)), ((), ())), preferred_element_type=jnp.float32
    )


def contract_cols(left_side, right_side):
    return lax.dot_general(
        left_side, right_side, (((1,), (1,)), ((), ())), preferred_element_type=jnp.float32
    )


def pick_block(blocks, block_index):
    return lax.dynamic_index_in_dim(blocks, block_index, 0, keepdims=False)


def gather_rows(chunks, tensor_count):
    n, c, d = chunks.shape
    spread = jnp.broadcast_to(chunks[:, None], (n, tensor_count, c, d))
    got = lax.all_to_all(spread, "tensor", 1, 1, tiled=False)
    return got.reshape(n, tensor_count * c, d)


def scatter_rows(parts, tensor_count):
    n, r, d = parts.shape
    split = parts.reshape(n, tensor_count, r // tensor_count, d)
    got = lax.all_to_all(split, "tensor", 1, 1, tiled=False)
    return jnp.sum(got.astype(jnp.float32), axis=1)


def swap_sites(block, flip):
    return lax.ppermute(block, "site", [(i, i ^ flip) for i in range(lax.axis_size("site"))])


def halving_site_sum(wide, axis):
    site_index = lax.axis_index("site")
    core_bit = site_index % 2
    chip_bit = site_index // 2
    half = wide.shape[axis] // 2
    quarter = half // 2

    def cut(block, start, size):
        return lax.dynamic_slice_in_dim(block, start, size, axis=axis)

    def join(first, second):
        return jnp.concatenate([first, second], axis=axis)

    sent = cut(wide, (1 - core_bit) * half, half).astype(jnp.bfloat16)
    kept = cut(wide, core_bit * half, half)
    pair_sum = kept + swap_sites(sent, 1).astype(jnp.float32)
    sent = cut(pair_sum, (1 - chip_bit) * quarter, quarter).astype(jnp.bfloat16)
    kept = cut(pair_sum, chip_bit * quarter, quarter)
    own = (kept + swap_sites(sent, 2).astype(jnp.float32)).astype(jnp.bfloat16)
    other = swap_sites(own, 2)
    own = jnp.where(chip_bit == 0, join(own, other), join(other, own))
    other = swap_sites(own, 1)
    whole = jnp.where(core_bit == 0, join(own, other), join(other, own))
    return whole.astype(jnp.float32)

def shards(
    inputs,
    out_grad,
    local_gate,
    local_up,
    local_down,
    local_gain,
    anchor_gate,
    anchor_up,
    anchor_down,
    anchor_gain,
):
    w_gate = local_gate[0, 0]
    w_up = local_up[0, 0]
    w_down = local_down[0, 0]
    gain_row = local_gain[0, 0]
    site_feed = inputs[0]
    loss_grad = out_grad[0]
    micro_count = site_feed.shape[0]
    row_count = site_feed.shape[1]
    feature_count = site_feed.shape[2]
    section_count = lax.axis_size("section")
    section_index = lax.axis_index("section")
    tensor_count = lax.axis_size("tensor")
    tensor_index = lax.axis_index("tensor")
    site_count = lax.axis_size("site")
    chunk = row_count // tensor_count
    row_start = tensor_index * chunk
    back_lag = 2 * (section_count - 1)
    tick_count = micro_count + back_lag
    last_fwd_tick = micro_count + section_count - 3
    first_bwd_tick = section_count - 1

    def my_rows(rows):
        return lax.dynamic_slice_in_dim(rows, row_start, chunk, axis=0)

    def hidden_of(normed):
        gate_pre = jnp.dot(normed, w_gate, preferred_element_type=jnp.float32)
        up_pre = jnp.dot(normed, w_up, preferred_element_type=jnp.float32)
        return (gate_pre, up_pre, jax.nn.sigmoid(gate_pre))

    def slot_of(micro_index):
        is_valid = (micro_index >= 0) & (micro_index < micro_count)
        return (is_valid, jnp.clip(micro_index, 0, micro_count - 1))

    weight_grads = (
        jnp.zeros(w_gate.shape, jnp.float32),
        jnp.zeros(w_up.shape, jnp.float32),
        jnp.zeros(w_gate.shape, jnp.float32),
    )
    hidden_count = w_gate.shape[1]
    gain_grad = jnp.zeros((feature_count,), jnp.float32)
    slots = micro_count + 1
    stored_chunk = jnp.zeros((slots, chunk, feature_count), jnp.bfloat16)
    stored_normed = jnp.zeros((slots, row_count, feature_count), jnp.bfloat16)
    stored_gate = jnp.zeros((slots, row_count, hidden_count), jnp.float32)
    stored_up = jnp.zeros((slots, row_count, hidden_count), jnp.float32)
    recv_fwd = jnp.zeros((chunk, feature_count), jnp.bfloat16)
    recv_bwd = jnp.zeros((chunk, feature_count), jnp.bfloat16)

    def keep(stack, value, slot):
        return lax.dynamic_update_index_in_dim(stack, value, slot, 0)

    for moment in range(tick_count):
        do_fwd = moment <= last_fwd_tick + 1
        do_bwd = moment >= first_bwd_tick
        fwd_valid, fwd_slot = slot_of(moment - section_index)
        fwd_slot = jnp.where(fwd_valid, fwd_slot, micro_count)
        bwd_valid, bwd_slot = slot_of(moment - back_lag + section_index)
        pieces = []
        if do_fwd:
            if moment < micro_count:
                fwd_chunk = jnp.where(section_index == 0, my_rows(site_feed[moment]), recv_fwd)
            else:
                fwd_chunk = recv_fwd
            pieces.append(fwd_chunk)
        if do_bwd:
            own_grad = my_rows(pick_block(loss_grad, bwd_slot))
            bwd_chunk = jnp.where(section_index == section_count - 1, own_grad, recv_bwd)
            bwd_chunk = jnp.where(bwd_valid, bwd_chunk, jnp.zeros_like(bwd_chunk))
            pieces.append(bwd_chunk)
        if moment == 0:
            gathered = [site_feed[0]]
        else:
            gathered_all = gather_rows(jnp.stack(pieces), tensor_count)
            gathered = [gathered_all[i] for i in range(len(pieces))]
        parts = []
        if do_fwd:
            wide_in = gathered[0].astype(jnp.float32)
            unit_rows, row_scale, normed = norm_rows(wide_in, gain_row)
            make_gate_pre, make_up_pre, make_sig_gate = hidden_of(normed)
            stored_chunk = keep(stored_chunk, fwd_chunk, fwd_slot)
            stored_normed = keep(stored_normed, normed, fwd_slot)
            stored_gate = keep(stored_gate, make_gate_pre, fwd_slot)
            stored_up = keep(stored_up, make_up_pre, fwd_slot)
        if do_fwd and moment <= last_fwd_tick:
            partial_value = jnp.dot(
                (make_gate_pre * make_sig_gate * make_up_pre).astype(jnp.bfloat16),
                w_down,
                preferred_element_type=jnp.float32,
            )
            parts.append(partial_value.astype(jnp.bfloat16))
        if do_bwd:
            incoming = gathered[-1]
            normed = pick_block(stored_normed, bwd_slot)
            local_gate_pre = pick_block(stored_gate, bwd_slot)
            local_up_pre = pick_block(stored_up, bwd_slot)
            sig_gate = jax.nn.sigmoid(local_gate_pre)
            silu_gate = local_gate_pre * sig_gate
            hidden = (silu_gate * local_up_pre).astype(jnp.bfloat16)
            d_hidden = contract_cols(incoming, w_down)
            d_gate_pre = (
                d_hidden * local_up_pre * sig_gate * (1.0 + local_gate_pre * (1.0 - sig_gate))
            ).astype(jnp.bfloat16)
            d_up_pre = (d_hidden * silu_gate).astype(jnp.bfloat16)
            weight_grads = (
                weight_grads[0] + contract_rows(normed, d_gate_pre),
                weight_grads[1] + contract_rows(normed, d_up_pre),
                weight_grads[2] + contract_rows(incoming, hidden),
            )
            d_part = contract_cols(d_gate_pre, w_gate) + contract_cols(d_up_pre, w_up)
            parts.append(d_part.astype(jnp.bfloat16))
        reduced = scatter_rows(jnp.stack(parts), tensor_count)
        if do_fwd and moment <= last_fwd_tick:
            out_chunk = (fwd_chunk.astype(jnp.float32) + reduced[0]).astype(jnp.bfloat16)
            recv_fwd = passed_along(out_chunk, "section", 1)
        if do_bwd:
            d_norm = reduced[-1]
            unit_mine, scale_mine, _ = norm_rows(
                pick_block(stored_chunk, bwd_slot).astype(jnp.float32), gain_row
            )
            gain_grad = gain_grad + jnp.sum(d_norm * unit_mine, axis=0)
            if moment + 1 < tick_count:
                d_unit = d_norm * gain_row
                sent_back = (
                    bwd_chunk.astype(jnp.float32)
                    + scale_mine
                    * (d_unit - unit_mine * jnp.mean(d_unit * unit_mine, axis=-1, keepdims=True))
                ).astype(jnp.bfloat16)
                recv_bwd = passed_along(sent_back, "section", -1)
    gain_term = gain_grad + jnp.where(
        tensor_index == 0, prox_weight * (gain_row - anchor_gain[0]), jnp.zeros_like(gain_row)
    )
    gate_term = weight_grads[0] + prox_weight * (
        w_gate.astype(jnp.float32) - anchor_gate[0].astype(jnp.float32)
    )
    up_term = weight_grads[1] + prox_weight * (
        w_up.astype(jnp.float32) - anchor_up[0].astype(jnp.float32)
    )
    down_term = weight_grads[2] + prox_weight * (
        w_down.astype(jnp.float32).T - anchor_down[0].astype(jnp.float32).T
    )
    totals = halving_site_sum(jnp.stack([gate_term, up_term, down_term]), 1)
    gate_total, up_total, down_total = (totals[0], totals[1], totals[2].T)
    group_count = site_count * tensor_count
    gain_spread = jnp.broadcast_to(gain_term[None], (group_count, feature_count))
    gain_total = jnp.sum(lax.all_to_all(gain_spread, ("site", "tensor"), 0, 0, tiled=False), axis=0)
    return (
        (gate_total / site_count)[None],
        (up_total / site_count)[None],
        (down_total / site_count)[None],
        (gain_total / site_count)[None],
    )


def solution(mesh):
    in_specs = (
        P("site", None, None, None),
        P("site", None, None, None),
        P("site", "section", None, "tensor"),
        P("site", "section", None, "tensor"),
        P("site", "section", "tensor", None),
        P("site", "section", None),
        P("section", None, "tensor"),
        P("section", None, "tensor"),
        P("section", "tensor", None),
        P("section", None),
    )
    out_specs = (
        P("section", None, "tensor"),
        P("section", None, "tensor"),
        P("section", "tensor", None),
        P("section", None),
    )
    return jax.shard_map(shards, mesh=mesh, in_specs=in_specs, out_specs=out_specs, check_vma=False)
```

```python
import jax
import jax.numpy as jnp
from jax import lax
from jax.sharding import PartitionSpec as P

epsilon = 1e-06
prox_weight = 1.0


def passed_along(block, axis, distance):
    devices = range(lax.axis_size(axis))
    route = [(i - distance, i) for i in devices if i - distance in devices]
    return lax.ppermute(block, axis, route)


def norm_rows(wide_rows, gain_row):
    row_scale = lax.rsqrt(jnp.mean(wide_rows * wide_rows, axis=-1, keepdims=True) + epsilon)
    unit_rows = wide_rows * row_scale
    return (unit_rows, row_scale, (unit_rows * gain_row).astype(jnp.bfloat16))


def contract_rows(left_side, right_side):
    return lax.dot_general(
        left_side, right_side, (((0,), (0,)), ((), ())), preferred_element_type=jnp.float32
    )


def contract_cols(left_side, right_side):
    return lax.dot_general(
        left_side, right_side, (((1,), (1,)), ((), ())), preferred_element_type=jnp.float32
    )


def pick_block(blocks, block_index):
    return lax.dynamic_index_in_dim(blocks, block_index, 0, keepdims=False)


def gather_rows(chunks, tensor_count):
    n, c, d = chunks.shape
    spread = jnp.broadcast_to(chunks[:, None], (n, tensor_count, c, d))
    got = lax.all_to_all(spread, "tensor", 1, 1, tiled=False)
    return got.reshape(n, tensor_count * c, d)


def scatter_rows(parts, tensor_count):
    n, r, d = parts.shape
    split = parts.reshape(n, tensor_count, r // tensor_count, d)
    got = lax.all_to_all(split, "tensor", 1, 1, tiled=False)
    return jnp.sum(got.astype(jnp.float32), axis=1)


def swap_sites(block, flip):
    return lax.ppermute(block, "site", [(i, i ^ flip) for i in range(lax.axis_size("site"))])


def halving_site_sum(wide):
    site_index = lax.axis_index("site")
    core_bit = site_index % 2
    chip_bit = site_index // 2
    half = wide.shape[0] // 2
    quarter = half // 2
    sent = lax.dynamic_slice_in_dim(wide, (1 - core_bit) * half, half).astype(jnp.bfloat16)
    kept = lax.dynamic_slice_in_dim(wide, core_bit * half, half)
    pair_sum = kept + swap_sites(sent, 1).astype(jnp.float32)
    sent = lax.dynamic_slice_in_dim(pair_sum, (1 - chip_bit) * quarter, quarter).astype(jnp.bfloat16)
    kept = lax.dynamic_slice_in_dim(pair_sum, chip_bit * quarter, quarter)
    own = (kept + swap_sites(sent, 2).astype(jnp.float32)).astype(jnp.bfloat16)
    other = swap_sites(own, 2)
    own = jnp.where(chip_bit == 0, jnp.concatenate([own, other]), jnp.concatenate([other, own]))
    other = swap_sites(own, 1)
    whole = jnp.where(core_bit == 0, jnp.concatenate([own, other]), jnp.concatenate([other, own]))
    return whole.astype(jnp.float32)


def shards(
    inputs,
    out_grad,
    local_gate,
    local_up,
    local_down,
    local_gain,
    anchor_gate,
    anchor_up,
    anchor_down,
    anchor_gain,
):
    w_gate = local_gate[0, 0]
    w_up = local_up[0, 0]
    w_down = local_down[0, 0]
    gain_row = local_gain[0, 0]
    site_feed = inputs[0]
    loss_grad = out_grad[0]
    micro_count = site_feed.shape[0]
    row_count = site_feed.shape[1]
    feature_count = site_feed.shape[2]
    section_count = lax.axis_size("section")
    section_index = lax.axis_index("section")
    tensor_count = lax.axis_size("tensor")
    tensor_index = lax.axis_index("tensor")
    site_count = lax.axis_size("site")
    chunk = row_count // tensor_count
    row_start = tensor_index * chunk
    back_lag = 2 * (section_count - 1)
    tick_count = micro_count + back_lag
    last_fwd_tick = micro_count + section_count - 3
    first_bwd_tick = section_count - 1

    def my_rows(rows):
        return lax.dynamic_slice_in_dim(rows, row_start, chunk, axis=0)

    def hidden_of(normed):
        gate_pre = jnp.dot(normed, w_gate, preferred_element_type=jnp.float32)
        up_pre = jnp.dot(normed, w_up, preferred_element_type=jnp.float32)
        return (gate_pre, up_pre, jax.nn.sigmoid(gate_pre))

    def slot_of(micro_index):
        is_valid = (micro_index >= 0) & (micro_index < micro_count)
        return (is_valid, jnp.clip(micro_index, 0, micro_count - 1))

    weight_grads = (
        jnp.zeros(w_gate.shape[::-1], jnp.float32),
        jnp.zeros(w_up.shape[::-1], jnp.float32),
        jnp.zeros(w_down.shape, jnp.float32),
    )
    hidden_count = w_gate.shape[1]
    gain_grad = jnp.zeros((feature_count,), jnp.float32)
    slots = micro_count + 1
    stored_chunk = jnp.zeros((slots, chunk, feature_count), jnp.bfloat16)
    stored_normed = jnp.zeros((slots, row_count, feature_count), jnp.bfloat16)
    stored_gate = jnp.zeros((slots, row_count, hidden_count), jnp.float32)
    stored_up = jnp.zeros((slots, row_count, hidden_count), jnp.float32)
    recv_fwd = jnp.zeros((chunk, feature_count), jnp.bfloat16)
    recv_bwd = jnp.zeros((chunk, feature_count), jnp.bfloat16)

    def keep(stack, value, slot):
        return lax.dynamic_update_index_in_dim(stack, value, slot, 0)

    for moment in range(tick_count):
        do_fwd = moment <= last_fwd_tick + 1
        do_bwd = moment >= first_bwd_tick
        fwd_valid, fwd_slot = slot_of(moment - section_index)
        fwd_slot = jnp.where(fwd_valid, fwd_slot, micro_count)
        bwd_valid, bwd_slot = slot_of(moment - back_lag + section_index)
        pieces = []
        if do_fwd:
            if moment < micro_count:
                fwd_chunk = jnp.where(section_index == 0, my_rows(site_feed[moment]), recv_fwd)
            else:
                fwd_chunk = recv_fwd
            pieces.append(fwd_chunk)
        if do_bwd:
            own_grad = my_rows(pick_block(loss_grad, bwd_slot))
            bwd_chunk = jnp.where(section_index == section_count - 1, own_grad, recv_bwd)
            bwd_chunk = jnp.where(bwd_valid, bwd_chunk, jnp.zeros_like(bwd_chunk))
            pieces.append(bwd_chunk)
        if moment == 0:
            gathered = [site_feed[0]]
        else:
            gathered_all = gather_rows(jnp.stack(pieces), tensor_count)
            gathered = [gathered_all[i] for i in range(len(pieces))]
        parts = []
        if do_fwd:
            wide_in = gathered[0].astype(jnp.float32)
            unit_rows, row_scale, normed = norm_rows(wide_in, gain_row)
            make_gate_pre, make_up_pre, make_sig_gate = hidden_of(normed)
            stored_chunk = keep(stored_chunk, fwd_chunk, fwd_slot)
            stored_normed = keep(stored_normed, normed, fwd_slot)
            stored_gate = keep(stored_gate, make_gate_pre, fwd_slot)
            stored_up = keep(stored_up, make_up_pre, fwd_slot)
        if do_fwd and moment <= last_fwd_tick:
            partial_value = jnp.dot(
                (make_gate_pre * make_sig_gate * make_up_pre).astype(jnp.bfloat16),
                w_down,
                preferred_element_type=jnp.float32,
            )
            parts.append(partial_value.astype(jnp.bfloat16))
        if do_bwd:
            incoming = gathered[-1]
            normed = pick_block(stored_normed, bwd_slot)
            local_gate_pre = pick_block(stored_gate, bwd_slot)
            local_up_pre = pick_block(stored_up, bwd_slot)
            sig_gate = jax.nn.sigmoid(local_gate_pre)
            silu_gate = local_gate_pre * sig_gate
            hidden = (silu_gate * local_up_pre).astype(jnp.bfloat16)
            d_hidden = contract_cols(incoming, w_down)
            d_gate_pre = (
                d_hidden * local_up_pre * sig_gate * (1.0 + local_gate_pre * (1.0 - sig_gate))
            ).astype(jnp.bfloat16)
            d_up_pre = (d_hidden * silu_gate).astype(jnp.bfloat16)
            weight_grads = (
                weight_grads[0] + contract_rows(d_gate_pre, normed),
                weight_grads[1] + contract_rows(d_up_pre, normed),
                weight_grads[2] + contract_rows(hidden, incoming),
            )
            d_part = contract_cols(d_gate_pre, w_gate) + contract_cols(d_up_pre, w_up)
            parts.append(d_part.astype(jnp.bfloat16))
        reduced = scatter_rows(jnp.stack(parts), tensor_count)
        if do_fwd and moment <= last_fwd_tick:
            out_chunk = (fwd_chunk.astype(jnp.float32) + reduced[0]).astype(jnp.bfloat16)
            recv_fwd = passed_along(out_chunk, "section", 1)
        if do_bwd:
            d_norm = reduced[-1]
            unit_mine, scale_mine, _ = norm_rows(
                pick_block(stored_chunk, bwd_slot).astype(jnp.float32), gain_row
            )
            gain_grad = gain_grad + jnp.sum(d_norm * unit_mine, axis=0)
            if moment + 1 < tick_count:
                d_unit = d_norm * gain_row
                sent_back = (
                    bwd_chunk.astype(jnp.float32)
                    + scale_mine
                    * (d_unit - unit_mine * jnp.mean(d_unit * unit_mine, axis=-1, keepdims=True))
                ).astype(jnp.bfloat16)
                recv_bwd = passed_along(sent_back, "section", -1)
    gain_term = gain_grad + jnp.where(
        tensor_index == 0, prox_weight * (gain_row - anchor_gain[0]), jnp.zeros_like(gain_row)
    )
    gate_term = weight_grads[0] + prox_weight * (
        w_gate.astype(jnp.float32).T - anchor_gate[0].astype(jnp.float32).T
    )
    up_term = weight_grads[1] + prox_weight * (
        w_up.astype(jnp.float32).T - anchor_up[0].astype(jnp.float32).T
    )
    down_term = weight_grads[2] + prox_weight * (
        w_down.astype(jnp.float32) - anchor_down[0].astype(jnp.float32)
    )
    gate_total, up_total, down_total = (
        halving_site_sum(gate_term).T,
        halving_site_sum(up_term).T,
        halving_site_sum(down_term),
    )
    group_count = site_count * tensor_count
    gain_spread = jnp.broadcast_to(gain_term[None], (group_count, feature_count))
    gain_total = jnp.sum(lax.all_to_all(gain_spread, ("site", "tensor"), 0, 0, tiled=False), axis=0)
    return (
        (gate_total / site_count)[None],
        (up_total / site_count)[None],
        (down_total / site_count)[None],
        (gain_total / site_count)[None],
    )


def solution(mesh):
    in_specs = (
        P("site", None, None, None),
        P("site", None, None, None),
        P("site", "section", None, "tensor"),
        P("site", "section", None, "tensor"),
        P("site", "section", "tensor", None),
        P("site", "section", None),
        P("section", None, "tensor"),
        P("section", None, "tensor"),
        P("section", "tensor", None),
        P("section", None),
    )
    out_specs = (
        P("section", None, "tensor"),
        P("section", None, "tensor"),
        P("section", "tensor", None),
        P("section", None),
    )
    return jax.shard_map(shards, mesh=mesh, in_specs=in_specs, out_specs=out_specs, check_vma=False)
```

```python
import jax
import jax.numpy as jnp
from jax import lax
from jax.sharding import PartitionSpec as P

epsilon = 1e-06
prox_weight = 1.0


def passed_along(block, axis, distance):
    devices = range(lax.axis_size(axis))
    route = [(i - distance, i) for i in devices if i - distance in devices]
    return lax.ppermute(block, axis, route)


def norm_rows(wide_rows, gain_row):
    row_scale = lax.rsqrt(jnp.mean(wide_rows * wide_rows, axis=-1, keepdims=True) + epsilon)
    unit_rows = wide_rows * row_scale
    return (unit_rows, row_scale, (unit_rows * gain_row).astype(jnp.bfloat16))


def contract_rows(left_side, right_side):
    return lax.dot_general(
        left_side, right_side, (((0,), (0,)), ((), ())), preferred_element_type=jnp.float32
    )


def contract_cols(left_side, right_side):
    return lax.dot_general(
        left_side, right_side, (((1,), (1,)), ((), ())), preferred_element_type=jnp.float32
    )


def pick_block(blocks, block_index):
    return lax.dynamic_index_in_dim(blocks, block_index, 0, keepdims=False)


def gather_rows(chunks, tensor_count):
    n, c, d = chunks.shape
    spread = jnp.broadcast_to(chunks[:, None], (n, tensor_count, c, d))
    got = lax.all_to_all(spread, "tensor", 1, 1, tiled=False)
    return got.reshape(n, tensor_count * c, d)


def scatter_rows(parts, tensor_count):
    n, r, d = parts.shape
    split = parts.reshape(n, tensor_count, r // tensor_count, d)
    got = lax.all_to_all(split, "tensor", 1, 1, tiled=False)
    return jnp.sum(got.astype(jnp.float32), axis=1)


def swap_sites(block, flip):
    return lax.ppermute(block, "site", [(i, i ^ flip) for i in range(lax.axis_size("site"))])


def halving_site_sum(wide):
    site_index = lax.axis_index("site")
    core_bit = site_index % 2
    chip_bit = site_index // 2
    half = wide.shape[0] // 2
    quarter = half // 2
    sent = lax.dynamic_slice_in_dim(wide, (1 - core_bit) * half, half).astype(jnp.bfloat16)
    kept = lax.dynamic_slice_in_dim(wide, core_bit * half, half)
    pair_sum = kept + swap_sites(sent, 1).astype(jnp.float32)
    sent = lax.dynamic_slice_in_dim(pair_sum, (1 - chip_bit) * quarter, quarter).astype(jnp.bfloat16)
    kept = lax.dynamic_slice_in_dim(pair_sum, chip_bit * quarter, quarter)
    own = (kept + swap_sites(sent, 2).astype(jnp.float32)).astype(jnp.bfloat16)
    other = swap_sites(own, 2)
    own = jnp.where(chip_bit == 0, jnp.concatenate([own, other]), jnp.concatenate([other, own]))
    other = swap_sites(own, 1)
    whole = jnp.where(core_bit == 0, jnp.concatenate([own, other]), jnp.concatenate([other, own]))
    return whole.astype(jnp.float32)


def shards(
    inputs,
    out_grad,
    local_gate,
    local_up,
    local_down,
    local_gain,
    anchor_gate,
    anchor_up,
    anchor_down,
    anchor_gain,
):
    w_gate = local_gate[0, 0]
    w_up = local_up[0, 0]
    w_down = local_down[0, 0]
    gain_row = local_gain[0, 0]
    site_feed = inputs[0]
    loss_grad = out_grad[0]
    micro_count = site_feed.shape[0]
    row_count = site_feed.shape[1]
    feature_count = site_feed.shape[2]
    section_count = lax.axis_size("section")
    section_index = lax.axis_index("section")
    tensor_count = lax.axis_size("tensor")
    tensor_index = lax.axis_index("tensor")
    site_count = lax.axis_size("site")
    chunk = row_count // tensor_count
    row_start = tensor_index * chunk
    back_lag = 2 * (section_count - 1)
    tick_count = micro_count + back_lag
    last_fwd_tick = micro_count + section_count - 3
    first_bwd_tick = section_count - 1

    def my_rows(rows):
        return lax.dynamic_slice_in_dim(rows, row_start, chunk, axis=0)

    def hidden_of(normed):
        gate_pre = jnp.dot(normed, w_gate, preferred_element_type=jnp.float32)
        up_pre = jnp.dot(normed, w_up, preferred_element_type=jnp.float32)
        return (gate_pre, up_pre, jax.nn.sigmoid(gate_pre))

    def slot_of(micro_index):
        is_valid = (micro_index >= 0) & (micro_index < micro_count)
        return (is_valid, jnp.clip(micro_index, 0, micro_count - 1))

    weight_grads = (
        jnp.zeros(w_gate.shape[::-1], jnp.float32),
        jnp.zeros(w_up.shape[::-1], jnp.float32),
        jnp.zeros(w_down.shape, jnp.float32),
    )
    hidden_count = w_gate.shape[1]
    gain_grad = jnp.zeros((feature_count,), jnp.float32)
    slots = micro_count + 1
    stored_chunk = jnp.zeros((slots, chunk, feature_count), jnp.bfloat16)
    stored_normed = jnp.zeros((slots, row_count, feature_count), jnp.bfloat16)
    stored_gate = jnp.zeros((slots, row_count, hidden_count), jnp.float32)
    stored_up = jnp.zeros((slots, row_count, hidden_count), jnp.float32)
    recv_fwd = jnp.zeros((chunk, feature_count), jnp.bfloat16)
    recv_bwd = jnp.zeros((chunk, feature_count), jnp.bfloat16)

    def keep(stack, value, slot):
        return lax.dynamic_update_index_in_dim(stack, value, slot, 0)

    for moment in range(tick_count):
        do_fwd = moment <= last_fwd_tick + 1
        do_bwd = moment >= first_bwd_tick
        fwd_valid, fwd_slot = slot_of(moment - section_index)
        fwd_slot = jnp.where(fwd_valid, fwd_slot, micro_count)
        bwd_valid, bwd_slot = slot_of(moment - back_lag + section_index)
        pieces = []
        if do_fwd:
            if moment < micro_count:
                fwd_chunk = jnp.where(section_index == 0, my_rows(site_feed[moment]), recv_fwd)
            else:
                fwd_chunk = recv_fwd
            pieces.append(fwd_chunk)
        if do_bwd:
            own_grad = my_rows(pick_block(loss_grad, bwd_slot))
            bwd_chunk = jnp.where(section_index == section_count - 1, own_grad, recv_bwd)
            bwd_chunk = jnp.where(bwd_valid, bwd_chunk, jnp.zeros_like(bwd_chunk))
            pieces.append(bwd_chunk)
        if moment == 0:
            gathered = [site_feed[0]]
        else:
            gathered_all = gather_rows(jnp.stack(pieces), tensor_count)
            gathered = [gathered_all[i] for i in range(len(pieces))]
        parts = []
        if do_fwd:
            wide_in = gathered[0].astype(jnp.float32)
            unit_rows, row_scale, normed = norm_rows(wide_in, gain_row)
            make_gate_pre, make_up_pre, make_sig_gate = hidden_of(normed)
            stored_chunk = keep(stored_chunk, fwd_chunk, fwd_slot)
            stored_normed = keep(stored_normed, normed, fwd_slot)
            stored_gate = keep(stored_gate, make_gate_pre, fwd_slot)
            stored_up = keep(stored_up, make_up_pre, fwd_slot)
        if do_fwd and moment <= last_fwd_tick:
            partial_value = jnp.dot(
                (make_gate_pre * make_sig_gate * make_up_pre).astype(jnp.bfloat16),
                w_down,
                preferred_element_type=jnp.float32,
            )
            parts.append(partial_value.astype(jnp.bfloat16))
        if do_bwd:
            incoming = gathered[-1]
            normed = pick_block(stored_normed, bwd_slot)
            local_gate_pre = pick_block(stored_gate, bwd_slot)
            local_up_pre = pick_block(stored_up, bwd_slot)
            sig_gate = jax.nn.sigmoid(local_gate_pre)
            silu_gate = local_gate_pre * sig_gate
            hidden = (silu_gate * local_up_pre).astype(jnp.bfloat16)
            d_hidden = contract_cols(incoming, w_down)
            d_gate_pre = (
                d_hidden * local_up_pre * sig_gate * (1.0 + local_gate_pre * (1.0 - sig_gate))
            ).astype(jnp.bfloat16)
            d_up_pre = (d_hidden * silu_gate).astype(jnp.bfloat16)
            weight_grads = (
                weight_grads[0] + contract_rows(d_gate_pre, normed),
                weight_grads[1] + contract_rows(d_up_pre, normed),
                weight_grads[2] + contract_rows(hidden, incoming),
            )
            d_part = contract_cols(d_gate_pre, w_gate) + contract_cols(d_up_pre, w_up)
            parts.append(d_part.astype(jnp.bfloat16))
        reduced = scatter_rows(jnp.stack(parts), tensor_count)
        if do_fwd and moment <= last_fwd_tick:
            out_chunk = (fwd_chunk.astype(jnp.float32) + reduced[0]).astype(jnp.bfloat16)
            recv_fwd = passed_along(out_chunk, "section", 1)
        if do_bwd:
            d_norm = reduced[-1]
            unit_mine, scale_mine, _ = norm_rows(
                pick_block(stored_chunk, bwd_slot).astype(jnp.float32), gain_row
            )
            gain_grad = gain_grad + jnp.sum(d_norm * unit_mine, axis=0)
            if moment + 1 < tick_count:
                d_unit = d_norm * gain_row
                sent_back = (
                    bwd_chunk.astype(jnp.float32)
                    + scale_mine
                    * (d_unit - unit_mine * jnp.mean(d_unit * unit_mine, axis=-1, keepdims=True))
                ).astype(jnp.bfloat16)
                recv_bwd = passed_along(sent_back, "section", -1)
    gain_term = gain_grad + jnp.where(
        tensor_index == 0, prox_weight * (gain_row - anchor_gain[0]), jnp.zeros_like(gain_row)
    )
    gate_term = weight_grads[0] + prox_weight * (
        w_gate.astype(jnp.float32).T - anchor_gate[0].astype(jnp.float32).T
    )
    up_term = weight_grads[1] + prox_weight * (
        w_up.astype(jnp.float32).T - anchor_up[0].astype(jnp.float32).T
    )
    down_term = weight_grads[2] + prox_weight * (
        w_down.astype(jnp.float32) - anchor_down[0].astype(jnp.float32)
    )
    gate_total, up_total, down_total = (
        halving_site_sum(gate_term / site_count).T,
        halving_site_sum(up_term / site_count).T,
        halving_site_sum(down_term / site_count),
    )
    group_count = site_count * tensor_count
    gain_spread = jnp.broadcast_to(gain_term[None], (group_count, feature_count))
    gain_total = jnp.sum(lax.all_to_all(gain_spread, ("site", "tensor"), 0, 0, tiled=False), axis=0)
    return (
        gate_total[None],
        up_total[None],
        down_total[None],
        (gain_total / site_count)[None],
    )


def solution(mesh):
    in_specs = (
        P("site", None, None, None),
        P("site", None, None, None),
        P("site", "section", None, "tensor"),
        P("site", "section", None, "tensor"),
        P("site", "section", "tensor", None),
        P("site", "section", None),
        P("section", None, "tensor"),
        P("section", None, "tensor"),
        P("section", "tensor", None),
        P("section", None),
    )
    out_specs = (
        P("section", None, "tensor"),
        P("section", None, "tensor"),
        P("section", "tensor", None),
        P("section", None),
    )
    return jax.shard_map(shards, mesh=mesh, in_specs=in_specs, out_specs=out_specs, check_vma=False)
```

```python
import jax
import jax.numpy as jnp
from jax import lax
from jax.sharding import PartitionSpec as P

epsilon = 1e-06
prox_weight = 1.0


def passed_along(block, axis, distance):
    devices = range(lax.axis_size(axis))
    route = [(i - distance, i) for i in devices if i - distance in devices]
    return lax.ppermute(block, axis, route)


def norm_rows(wide_rows, gain_row):
    row_scale = lax.rsqrt(jnp.mean(wide_rows * wide_rows, axis=-1, keepdims=True) + epsilon)
    unit_rows = wide_rows * row_scale
    return (unit_rows, row_scale, (unit_rows * gain_row).astype(jnp.bfloat16))


def contract_rows(left_side, right_side):
    return lax.dot_general(
        left_side, right_side, (((0,), (0,)), ((), ())), preferred_element_type=jnp.float32
    )


def contract_cols(left_side, right_side):
    return lax.dot_general(
        left_side, right_side, (((1,), (1,)), ((), ())), preferred_element_type=jnp.float32
    )


def pick_block(blocks, block_index):
    return lax.dynamic_index_in_dim(blocks, block_index, 0, keepdims=False)


def gather_rows(chunks, tensor_count):
    n, c, d = chunks.shape
    spread = jnp.broadcast_to(chunks[:, None], (n, tensor_count, c, d))
    got = lax.all_to_all(spread, "tensor", 1, 1, tiled=False)
    return got.reshape(n, tensor_count * c, d)


def scatter_rows(parts, tensor_count):
    n, r, d = parts.shape
    split = parts.reshape(n, tensor_count, r // tensor_count, d)
    got = lax.all_to_all(split, "tensor", 1, 1, tiled=False)
    return jnp.sum(got.astype(jnp.float32), axis=1)


def relay_both(ahead, behind, section_index, section_count):
    targets = jnp.arange(section_count)[:, None, None]
    zeros = jnp.zeros_like(ahead)
    spread = jnp.where(
        targets == section_index + 1,
        ahead[None],
        jnp.where(targets == section_index - 1, behind[None], zeros[None]),
    )
    got = lax.all_to_all(spread, "section", 0, 0, tiled=False)
    from_prev = pick_block(got, jnp.clip(section_index - 1, 0, section_count - 1))
    from_next = pick_block(got, jnp.clip(section_index + 1, 0, section_count - 1))
    from_prev = jnp.where(section_index > 0, from_prev, zeros)
    from_next = jnp.where(section_index < section_count - 1, from_next, zeros)
    return from_prev, from_next


def swap_sites(block, flip):
    return lax.ppermute(block, "site", [(i, i ^ flip) for i in range(lax.axis_size("site"))])


def halving_site_sum(wide):
    site_index = lax.axis_index("site")
    core_bit = site_index % 2
    chip_bit = site_index // 2
    half = wide.shape[0] // 2
    quarter = half // 2
    sent = lax.dynamic_slice_in_dim(wide, (1 - core_bit) * half, half).astype(jnp.bfloat16)
    kept = lax.dynamic_slice_in_dim(wide, core_bit * half, half)
    pair_sum = kept + swap_sites(sent, 1).astype(jnp.float32)
    sent = lax.dynamic_slice_in_dim(pair_sum, (1 - chip_bit) * quarter, quarter).astype(jnp.bfloat16)
    kept = lax.dynamic_slice_in_dim(pair_sum, chip_bit * quarter, quarter)
    own = (kept + swap_sites(sent, 2).astype(jnp.float32)).astype(jnp.bfloat16)
    other = swap_sites(own, 2)
    own = jnp.where(chip_bit == 0, jnp.concatenate([own, other]), jnp.concatenate([other, own]))
    other = swap_sites(own, 1)
    whole = jnp.where(core_bit == 0, jnp.concatenate([own, other]), jnp.concatenate([other, own]))
    return whole.astype(jnp.float32)


def shards(
    inputs,
    out_grad,
    local_gate,
    local_up,
    local_down,
    local_gain,
    anchor_gate,
    anchor_up,
    anchor_down,
    anchor_gain,
):
    w_gate = local_gate[0, 0]
    w_up = local_up[0, 0]
    w_down = local_down[0, 0]
    gain_row = local_gain[0, 0]
    site_feed = inputs[0]
    loss_grad = out_grad[0]
    micro_count = site_feed.shape[0]
    row_count = site_feed.shape[1]
    feature_count = site_feed.shape[2]
    section_count = lax.axis_size("section")
    section_index = lax.axis_index("section")
    tensor_count = lax.axis_size("tensor")
    tensor_index = lax.axis_index("tensor")
    site_count = lax.axis_size("site")
    chunk = row_count // tensor_count
    row_start = tensor_index * chunk
    back_lag = 2 * (section_count - 1)
    tick_count = micro_count + back_lag
    last_fwd_tick = micro_count + section_count - 3
    first_bwd_tick = section_count - 1

    def my_rows(rows):
        return lax.dynamic_slice_in_dim(rows, row_start, chunk, axis=0)

    def hidden_of(normed):
        gate_pre = jnp.dot(normed, w_gate, preferred_element_type=jnp.float32)
        up_pre = jnp.dot(normed, w_up, preferred_element_type=jnp.float32)
        return (gate_pre, up_pre, jax.nn.sigmoid(gate_pre))

    def slot_of(micro_index):
        is_valid = (micro_index >= 0) & (micro_index < micro_count)
        return (is_valid, jnp.clip(micro_index, 0, micro_count - 1))

    weight_grads = (
        jnp.zeros(w_gate.shape[::-1], jnp.float32),
        jnp.zeros(w_up.shape[::-1], jnp.float32),
        jnp.zeros(w_down.shape, jnp.float32),
    )
    hidden_count = w_gate.shape[1]
    gain_grad = jnp.zeros((feature_count,), jnp.float32)
    slots = micro_count + 1
    stored_chunk = jnp.zeros((slots, chunk, feature_count), jnp.bfloat16)
    stored_normed = jnp.zeros((slots, row_count, feature_count), jnp.bfloat16)
    stored_gate = jnp.zeros((slots, row_count, hidden_count), jnp.float32)
    stored_up = jnp.zeros((slots, row_count, hidden_count), jnp.float32)
    recv_fwd = jnp.zeros((chunk, feature_count), jnp.bfloat16)
    recv_bwd = jnp.zeros((chunk, feature_count), jnp.bfloat16)

    def keep(stack, value, slot):
        return lax.dynamic_update_index_in_dim(stack, value, slot, 0)

    for moment in range(tick_count):
        do_fwd = moment <= last_fwd_tick + 1
        do_bwd = moment >= first_bwd_tick
        fwd_valid, fwd_slot = slot_of(moment - section_index)
        fwd_slot = jnp.where(fwd_valid, fwd_slot, micro_count)
        bwd_valid, bwd_slot = slot_of(moment - back_lag + section_index)
        pieces = []
        if do_fwd:
            if moment < micro_count:
                fwd_chunk = jnp.where(section_index == 0, my_rows(site_feed[moment]), recv_fwd)
            else:
                fwd_chunk = recv_fwd
            pieces.append(fwd_chunk)
        if do_bwd:
            own_grad = my_rows(pick_block(loss_grad, bwd_slot))
            bwd_chunk = jnp.where(section_index == section_count - 1, own_grad, recv_bwd)
            bwd_chunk = jnp.where(bwd_valid, bwd_chunk, jnp.zeros_like(bwd_chunk))
            pieces.append(bwd_chunk)
        if moment == 0:
            gathered = [site_feed[0]]
        else:
            gathered_all = gather_rows(jnp.stack(pieces), tensor_count)
            gathered = [gathered_all[i] for i in range(len(pieces))]
        parts = []
        if do_fwd:
            wide_in = gathered[0].astype(jnp.float32)
            unit_rows, row_scale, normed = norm_rows(wide_in, gain_row)
            make_gate_pre, make_up_pre, make_sig_gate = hidden_of(normed)
            stored_chunk = keep(stored_chunk, fwd_chunk, fwd_slot)
            stored_normed = keep(stored_normed, normed, fwd_slot)
            stored_gate = keep(stored_gate, make_gate_pre, fwd_slot)
            stored_up = keep(stored_up, make_up_pre, fwd_slot)
        if do_fwd and moment <= last_fwd_tick:
            partial_value = jnp.dot(
                (make_gate_pre * make_sig_gate * make_up_pre).astype(jnp.bfloat16),
                w_down,
                preferred_element_type=jnp.float32,
            )
            parts.append(partial_value.astype(jnp.bfloat16))
        if do_bwd:
            incoming = gathered[-1]
            normed = pick_block(stored_normed, bwd_slot)
            local_gate_pre = pick_block(stored_gate, bwd_slot)
            local_up_pre = pick_block(stored_up, bwd_slot)
            sig_gate = jax.nn.sigmoid(local_gate_pre)
            silu_gate = local_gate_pre * sig_gate
            hidden = (silu_gate * local_up_pre).astype(jnp.bfloat16)
            d_hidden = contract_cols(incoming, w_down)
            d_gate_pre = (
                d_hidden * local_up_pre * sig_gate * (1.0 + local_gate_pre * (1.0 - sig_gate))
            ).astype(jnp.bfloat16)
            d_up_pre = (d_hidden * silu_gate).astype(jnp.bfloat16)
            weight_grads = (
                weight_grads[0] + contract_rows(d_gate_pre, normed),
                weight_grads[1] + contract_rows(d_up_pre, normed),
                weight_grads[2] + contract_rows(hidden, incoming),
            )
            d_part = contract_cols(d_gate_pre, w_gate) + contract_cols(d_up_pre, w_up)
            parts.append(d_part.astype(jnp.bfloat16))
        reduced = scatter_rows(jnp.stack(parts), tensor_count)
        both_ways = do_fwd and moment <= last_fwd_tick and do_bwd and moment + 1 < tick_count
        if do_fwd and moment <= last_fwd_tick:
            out_chunk = (fwd_chunk.astype(jnp.float32) + reduced[0]).astype(jnp.bfloat16)
            if not both_ways:
                recv_fwd = passed_along(out_chunk, "section", 1)
        if do_bwd:
            d_norm = reduced[-1]
            unit_mine, scale_mine, _ = norm_rows(
                pick_block(stored_chunk, bwd_slot).astype(jnp.float32), gain_row
            )
            gain_grad = gain_grad + jnp.sum(d_norm * unit_mine, axis=0)
            if moment + 1 < tick_count:
                d_unit = d_norm * gain_row
                sent_back = (
                    bwd_chunk.astype(jnp.float32)
                    + scale_mine
                    * (d_unit - unit_mine * jnp.mean(d_unit * unit_mine, axis=-1, keepdims=True))
                ).astype(jnp.bfloat16)
                if both_ways:
                    recv_fwd, recv_bwd = relay_both(out_chunk, sent_back, section_index, section_count)
                else:
                    recv_bwd = passed_along(sent_back, "section", -1)
    gain_term = gain_grad + jnp.where(
        tensor_index == 0, prox_weight * (gain_row - anchor_gain[0]), jnp.zeros_like(gain_row)
    )
    gate_term = weight_grads[0] + prox_weight * (
        w_gate.astype(jnp.float32).T - anchor_gate[0].astype(jnp.float32).T
    )
    up_term = weight_grads[1] + prox_weight * (
        w_up.astype(jnp.float32).T - anchor_up[0].astype(jnp.float32).T
    )
    down_term = weight_grads[2] + prox_weight * (
        w_down.astype(jnp.float32) - anchor_down[0].astype(jnp.float32)
    )
    gate_total, up_total, down_total = (
        halving_site_sum(gate_term).T,
        halving_site_sum(up_term).T,
        halving_site_sum(down_term),
    )
    group_count = site_count * tensor_count
    gain_spread = jnp.broadcast_to(gain_term[None], (group_count, feature_count))
    gain_total = jnp.sum(lax.all_to_all(gain_spread, ("site", "tensor"), 0, 0, tiled=False), axis=0)
    return (
        (gate_total / site_count)[None],
        (up_total / site_count)[None],
        (down_total / site_count)[None],
        (gain_total / site_count)[None],
    )


def solution(mesh):
    in_specs = (
        P("site", None, None, None),
        P("site", None, None, None),
        P("site", "section", None, "tensor"),
        P("site", "section", None, "tensor"),
        P("site", "section", "tensor", None),
        P("site", "section", None),
        P("section", None, "tensor"),
        P("section", None, "tensor"),
        P("section", "tensor", None),
        P("section", None),
    )
    out_specs = (
        P("section", None, "tensor"),
        P("section", None, "tensor"),
        P("section", "tensor", None),
        P("section", None),
    )
    return jax.shard_map(shards, mesh=mesh, in_specs=in_specs, out_specs=out_specs, check_vma=False)
```

```python
import jax
import jax.numpy as jnp
from jax import lax
from jax.sharding import PartitionSpec as P

epsilon = 1e-06
prox_weight = 1.0


def passed_along(block, axis, distance):
    devices = range(lax.axis_size(axis))
    route = [(i - distance, i) for i in devices if i - distance in devices]
    return lax.ppermute(block, axis, route)


def norm_rows(wide_rows, gain_row):
    row_scale = lax.rsqrt(jnp.mean(wide_rows * wide_rows, axis=-1, keepdims=True) + epsilon)
    unit_rows = wide_rows * row_scale
    return (unit_rows, row_scale, (unit_rows * gain_row).astype(jnp.bfloat16))


def contract_rows(left_side, right_side):
    return lax.dot_general(
        left_side, right_side, (((0,), (0,)), ((), ())), preferred_element_type=jnp.float32
    )


def contract_cols(left_side, right_side):
    return lax.dot_general(
        left_side, right_side, (((1,), (1,)), ((), ())), preferred_element_type=jnp.float32
    )


def pick_block(blocks, block_index):
    return lax.dynamic_index_in_dim(blocks, block_index, 0, keepdims=False)


def gather_rows(chunks, tensor_count):
    n, c, d = chunks.shape
    spread = jnp.broadcast_to(chunks[:, None], (n, tensor_count, c, d))
    got = lax.all_to_all(spread, "tensor", 1, 1, tiled=False)
    return got.reshape(n, tensor_count * c, d)


def scatter_rows(parts, tensor_count):
    n, r, d = parts.shape
    split = parts.reshape(n, tensor_count, r // tensor_count, d)
    got = lax.all_to_all(split, "tensor", 1, 1, tiled=False)
    return jnp.sum(got.astype(jnp.float32), axis=1)


def swap_sites(block, flip):
    return lax.ppermute(block, "site", [(i, i ^ flip) for i in range(lax.axis_size("site"))])


def halving_site_sum(wide):
    site_index = lax.axis_index("site")
    core_bit = site_index % 2
    chip_bit = site_index // 2
    half = wide.shape[0] // 2
    quarter = half // 2
    sent = lax.dynamic_slice_in_dim(wide, (1 - core_bit) * half, half).astype(jnp.bfloat16)
    kept = lax.dynamic_slice_in_dim(wide, core_bit * half, half)
    pair_sum = kept + swap_sites(sent, 1).astype(jnp.float32)
    sent = lax.dynamic_slice_in_dim(pair_sum, (1 - chip_bit) * quarter, quarter).astype(jnp.bfloat16)
    kept = lax.dynamic_slice_in_dim(pair_sum, chip_bit * quarter, quarter)
    own = (kept + swap_sites(sent, 2).astype(jnp.float32)).astype(jnp.bfloat16)
    other = swap_sites(own, 2)
    own = jnp.where(chip_bit == 0, jnp.concatenate([own, other]), jnp.concatenate([other, own]))
    other = swap_sites(own, 1)
    whole = jnp.where(core_bit == 0, jnp.concatenate([own, other]), jnp.concatenate([other, own]))
    return whole.astype(jnp.float32)


def shards(
    inputs,
    out_grad,
    local_gate,
    local_up,
    local_down,
    local_gain,
    anchor_gate,
    anchor_up,
    anchor_down,
    anchor_gain,
):
    w_gate = local_gate[0, 0]
    w_up = local_up[0, 0]
    w_down = local_down[0, 0]
    gain_row = local_gain[0, 0]
    site_feed = inputs[0]
    loss_grad = out_grad[0]
    micro_count = site_feed.shape[0]
    row_count = site_feed.shape[1]
    feature_count = site_feed.shape[2]
    section_count = lax.axis_size("section")
    section_index = lax.axis_index("section")
    tensor_count = lax.axis_size("tensor")
    tensor_index = lax.axis_index("tensor")
    site_count = lax.axis_size("site")
    chunk = row_count // tensor_count
    row_start = tensor_index * chunk
    back_lag = 2 * (section_count - 1)
    tick_count = micro_count + back_lag
    last_fwd_tick = micro_count + section_count - 3
    first_bwd_tick = section_count - 1

    def my_rows(rows):
        return lax.dynamic_slice_in_dim(rows, row_start, chunk, axis=0)

    def hidden_of(normed):
        gate_pre = jnp.dot(normed, w_gate, preferred_element_type=jnp.float32)
        up_pre = jnp.dot(normed, w_up, preferred_element_type=jnp.float32)
        return (gate_pre, up_pre, jax.nn.sigmoid(gate_pre))

    def slot_of(micro_index):
        is_valid = (micro_index >= 0) & (micro_index < micro_count)
        return (is_valid, jnp.clip(micro_index, 0, micro_count - 1))

    weight_grads = (
        jnp.zeros(w_gate.shape[::-1], jnp.float32),
        jnp.zeros(w_up.shape[::-1], jnp.float32),
        jnp.zeros(w_down.shape, jnp.float32),
    )
    hidden_count = w_gate.shape[1]
    gain_grad = jnp.zeros((feature_count,), jnp.float32)
    slots = micro_count + 1
    stored_chunk = jnp.zeros((slots, chunk, feature_count), jnp.bfloat16)
    stored_normed = jnp.zeros((slots, row_count, feature_count), jnp.bfloat16)
    stored_gate = jnp.zeros((slots, row_count, hidden_count), jnp.float32)
    stored_up = jnp.zeros((slots, row_count, hidden_count), jnp.float32)
    recv_fwd = jnp.zeros((chunk, feature_count), jnp.bfloat16)
    recv_bwd = jnp.zeros((chunk, feature_count), jnp.bfloat16)

    def keep(stack, value, slot):
        return lax.dynamic_update_index_in_dim(stack, value, slot, 0)

    for moment in range(tick_count):
        do_fwd = moment <= last_fwd_tick + 1
        do_bwd = moment >= first_bwd_tick
        fwd_valid, fwd_slot = slot_of(moment - section_index)
        fwd_slot = jnp.where(fwd_valid, fwd_slot, micro_count)
        bwd_valid, bwd_slot = slot_of(moment - back_lag + section_index)
        pieces = []
        if do_fwd:
            if moment < micro_count:
                fwd_chunk = jnp.where(section_index == 0, my_rows(site_feed[moment]), recv_fwd)
            else:
                fwd_chunk = recv_fwd
            pieces.append(fwd_chunk)
        if do_bwd:
            own_grad = my_rows(pick_block(loss_grad, bwd_slot))
            bwd_chunk = jnp.where(section_index == section_count - 1, own_grad, recv_bwd)
            bwd_chunk = jnp.where(bwd_valid, bwd_chunk, jnp.zeros_like(bwd_chunk))
            pieces.append(bwd_chunk)
        if moment == 0:
            gathered = [site_feed[0]]
        else:
            gathered_all = gather_rows(jnp.stack(pieces), tensor_count)
            gathered = [gathered_all[i] for i in range(len(pieces))]
        parts = []
        if do_fwd:
            wide_in = gathered[0].astype(jnp.float32)
            unit_rows, row_scale, normed = norm_rows(wide_in, gain_row)
            make_gate_pre, make_up_pre, make_sig_gate = hidden_of(normed)
            stored_chunk = keep(stored_chunk, fwd_chunk, fwd_slot)
            stored_normed = keep(stored_normed, normed, fwd_slot)
            stored_gate = keep(stored_gate, make_gate_pre, fwd_slot)
            stored_up = keep(stored_up, make_up_pre, fwd_slot)
        if do_fwd and moment <= last_fwd_tick:
            partial_value = jnp.dot(
                (make_gate_pre * make_sig_gate * make_up_pre).astype(jnp.bfloat16),
                w_down,
                preferred_element_type=jnp.float32,
            )
            parts.append(partial_value.astype(jnp.bfloat16))
        if do_bwd:
            incoming = gathered[-1]
            normed = pick_block(stored_normed, bwd_slot)
            local_gate_pre = pick_block(stored_gate, bwd_slot)
            local_up_pre = pick_block(stored_up, bwd_slot)
            sig_gate = jax.nn.sigmoid(local_gate_pre)
            silu_gate = local_gate_pre * sig_gate
            hidden = (silu_gate * local_up_pre).astype(jnp.bfloat16)
            d_hidden = contract_cols(incoming, w_down)
            d_gate_pre = (
                d_hidden * local_up_pre * sig_gate * (1.0 + local_gate_pre * (1.0 - sig_gate))
            ).astype(jnp.bfloat16)
            d_up_pre = (d_hidden * silu_gate).astype(jnp.bfloat16)
            weight_grads = (
                weight_grads[0] + contract_rows(d_gate_pre, normed),
                weight_grads[1] + contract_rows(d_up_pre, normed),
                weight_grads[2] + contract_rows(hidden, incoming),
            )
            d_part = contract_cols(d_gate_pre, w_gate) + contract_cols(d_up_pre, w_up)
            parts.append(d_part.astype(jnp.bfloat16))
        if moment + 1 == tick_count:
            last_unit, _, _ = norm_rows(site_feed[micro_count - 1].astype(jnp.float32), gain_row)
            gain_grad = gain_grad + jnp.sum(parts[-1].astype(jnp.float32) * last_unit, axis=0)
            continue
        reduced = scatter_rows(jnp.stack(parts), tensor_count)
        if do_fwd and moment <= last_fwd_tick:
            out_chunk = (fwd_chunk.astype(jnp.float32) + reduced[0]).astype(jnp.bfloat16)
            recv_fwd = passed_along(out_chunk, "section", 1)
        if do_bwd:
            d_norm = reduced[-1]
            unit_mine, scale_mine, _ = norm_rows(
                pick_block(stored_chunk, bwd_slot).astype(jnp.float32), gain_row
            )
            gain_grad = gain_grad + jnp.sum(d_norm * unit_mine, axis=0)
            if moment + 1 < tick_count:
                d_unit = d_norm * gain_row
                sent_back = (
                    bwd_chunk.astype(jnp.float32)
                    + scale_mine
                    * (d_unit - unit_mine * jnp.mean(d_unit * unit_mine, axis=-1, keepdims=True))
                ).astype(jnp.bfloat16)
                recv_bwd = passed_along(sent_back, "section", -1)
    gain_term = gain_grad + jnp.where(
        tensor_index == 0, prox_weight * (gain_row - anchor_gain[0]), jnp.zeros_like(gain_row)
    )
    gate_term = weight_grads[0] + prox_weight * (
        w_gate.astype(jnp.float32).T - anchor_gate[0].astype(jnp.float32).T
    )
    up_term = weight_grads[1] + prox_weight * (
        w_up.astype(jnp.float32).T - anchor_up[0].astype(jnp.float32).T
    )
    down_term = weight_grads[2] + prox_weight * (
        w_down.astype(jnp.float32) - anchor_down[0].astype(jnp.float32)
    )
    gate_total, up_total, down_total = (
        halving_site_sum(gate_term).T,
        halving_site_sum(up_term).T,
        halving_site_sum(down_term),
    )
    group_count = site_count * tensor_count
    gain_spread = jnp.broadcast_to(gain_term[None], (group_count, feature_count))
    gain_total = jnp.sum(lax.all_to_all(gain_spread, ("site", "tensor"), 0, 0, tiled=False), axis=0)
    return (
        (gate_total / site_count)[None],
        (up_total / site_count)[None],
        (down_total / site_count)[None],
        (gain_total / site_count)[None],
    )


def solution(mesh):
    in_specs = (
        P("site", None, None, None),
        P("site", None, None, None),
        P("site", "section", None, "tensor"),
        P("site", "section", None, "tensor"),
        P("site", "section", "tensor", None),
        P("site", "section", None),
        P("section", None, "tensor"),
        P("section", None, "tensor"),
        P("section", "tensor", None),
        P("section", None),
    )
    out_specs = (
        P("section", None, "tensor"),
        P("section", None, "tensor"),
        P("section", "tensor", None),
        P("section", None),
    )
    return jax.shard_map(shards, mesh=mesh, in_specs=in_specs, out_specs=out_specs, check_vma=False)
```
